256 devices in a mesh: member: 4 (over z_hi), token: 64 (over z_lo, x, y, core).
Axes of the slice: x: 4, y: 4, z: 8 (z_hi: 4, z_lo: 2; z = z_hi * 2 + z_lo), core: 2. Of those that a mesh axis runs over, the one named last changes fastest.
Arguments:
- members_in: bfloat16 [8, 8192, 1024], P('member', 'token'), may hold values from -16 to 16
- member_noise: bfloat16 [8, 8192, 1024], P('member', 'token'), may hold values from -6 to 6
- norm_gain: float32 [1024], replicated, may hold values from 0.25 to 1.75
- weight_query: bfloat16 [1024, 1024], replicated, may hold values from -0.1875 to 0.1875
- weight_key: bfloat16 [1024, 1024], replicated, may hold values from -0.1875 to 0.1875
- weight_value: bfloat16 [1024, 1024], replicated, may hold values from -0.1875 to 0.1875
- weight_out: bfloat16 [1024, 1024], replicated, may hold values from -0.1875 to 0.1875
- decoder_projection_weight: bfloat16 [100, 1024], replicated, may hold values from -0.1875 to 0.1875
- decoder_bias: float32 [100], replicated, may hold values from -3 to 3
- observations: float32 [100, 65536], P(None, 'token'), may hold values from -6 to 6
- surface_extent_factor: float32 [65536], P('token'), may hold values from 0.3 to 3
- quantity_scoring_factor: float32 [100], replicated, may hold values from 0.2 to 2
- point_map: int32 [65536], P('token'), may hold values from 0 to 127
Outputs:
- mean_scoring: float32 [], replicated
- grad_members: bfloat16 [8, 8192, 1024], P('member', 'token')
- grad_out: float32 [1024, 1024], P('token')
- grad_decoder: float32 [100, 1024], replicated
The draws below stay inside these ranges and needn't reach their ends.
Inputs may be any that keep to these rules, and one draw needn't show every extreme that they name: Point p belongs to token (p // 1024) * 128 + point_map[p].
All inputs are finite; a program needn't handle non-finite values.
Results may differ from the reference program's by a relative error of at most 0.015.
Values may be sent and summed in bfloat16 or wider, within the bound.
No kernel may reach another device: no remote copies, remote signals or barrier semaphores. Data moves between devices by JAX's collectives and lax.ppermute only.
A program may use at most 128 MiB of HBM per device.

```python
import math
import jax
import jax.numpy as jnp
from jax import lax

HEADS = 16
VARS = 100
HALF = 128
TOK_DEV = 128
C = 1024
SITES_EACH_PART = 1024
MEMBERS = 8
TOKENS = 8192
POINTS = 65536


def set_ends(values, key, least, top_value):
    place = [jax.random.randint(jax.random.fold_in(key, axis), (), 0, length) for axis, length in enumerate(values.shape)]
    main_axis = values.shape.index(max(values.shape))
    next_to = place[:main_axis] + [(place[main_axis] + 1) % values.shape[main_axis]] + place[main_axis + 1:]
    return values.at[tuple(place)].set(least).at[tuple(next_to)].set(top_value)


def with_spikes(result, rng, source, target, shards_of, factor):
    owner, partner = [(jnp.arange(result.shape[position]) // (result.shape[position] // shards_of)).reshape([-1 if axis == position else 1 for axis in range(result.ndim)]) for position in (source, target)]
    chosen = jax.random.permutation(rng, shards_of)[partner]
    strong = (owner == chosen) | (owner == (partner + shards_of // 2) % shards_of)
    return jnp.where(strong, factor * result, result)


def steps_of(stream_key, dims, shards, least, top_value):
    def one(position, blocks):
        heights = jax.random.uniform(jax.random.fold_in(jax.random.fold_in(stream_key, 6), position), (blocks,), jnp.float32, least / len(shards), top_value / len(shards))
        return jnp.repeat(jnp.exp(heights), dims[position] // blocks).reshape((-1,) + (1,) * (len(dims) - position - 1))

    level = one(*shards[0])
    for cut in shards[1:]:
        level = level * one(*cut)
    return level


def gaussian(stream_key, shape, scale, most, cuts=(), kind=jnp.bfloat16):
    entries = jax.random.normal(stream_key, shape, jnp.float32) * scale
    if len(cuts) > 0:
        entries = steps_of(stream_key, shape, cuts, -0.22, 0.18) * entries
    return jnp.clip(entries, min=-most, max=most).astype(kind)


def gaussian_with(rng, dims, deviation, most, shards, heavy, held_as=jnp.bfloat16):
    values = deviation * jax.random.normal(rng, dims, jnp.float32)
    if shards:
        values = values * steps_of(rng, dims, shards, -0.22, 0.18)
    return jnp.clip(with_spikes(values, jax.random.fold_in(rng, 3), *heavy), -most, most).astype(held_as)


def setup_inputs(seed: int = 0) -> dict:
    key_list = jax.random.split(jax.random.key(seed), 14)
    return {
        "members_in": gaussian_with(key_list[0], (MEMBERS, TOKENS, C), 1.0, 16.0, ((0, 4), (1, 64)), (1, 2, 64, 4.0)),
        "member_noise": gaussian(key_list[1], (MEMBERS, TOKENS, C), 1.0, 6.0, ((0, 4), (1, 64))),
        "norm_gain": jnp.clip(1.0 + 0.15 * jax.random.normal(key_list[2], (C,), jnp.float32), 0.25, 1.75),
        "weight_query": gaussian(key_list[3], (C, C), C ** -0.5, 0.1875),
        "weight_key": gaussian(key_list[4], (C, C), C ** -0.5, 0.1875),
        "weight_value": gaussian(key_list[5], (C, C), C ** -0.5, 0.1875),
        "weight_out": gaussian(key_list[6], (C, C), C ** -0.5, 0.1875),
        "decoder_projection_weight": gaussian(key_list[7], (VARS, C), C ** -0.5, 0.1875),
        "decoder_bias": gaussian(key_list[8], (VARS,), 0.5, 3.0, (), jnp.float32),
        "observations": gaussian(key_list[9], (VARS, POINTS), 1.0, 6.0, ((1, 64),), jnp.float32),
        "surface_extent_factor": jnp.clip(jnp.exp(math.log(3.0) - 2.3025851 * jax.random.uniform(key_list[10], (POINTS,), jnp.float32) ** steps_of(key_list[10], (POINTS,), ((0, 64),), -0.2, 0.2)), 0.3, 3.0),
        "quantity_scoring_factor": jnp.clip(jnp.exp(jax.random.uniform(key_list[11], (VARS,), jnp.float32, math.log(0.2), math.log(2.0))), 0.2, 2.0),
        "point_map": set_ends(jax.random.randint(key_list[12], (POINTS,), 0, TOK_DEV), jax.random.fold_in(key_list[12], 1), 0, TOK_DEV - 1).astype(jnp.int32),
    }


EPSILON = 1e-06
SMOOTH = 0.01

def normalize_heads(flat):
    rows, width = flat.shape
    split = flat.reshape(rows, HEADS, width // HEADS)
    split = split * lax.rsqrt(lax.optimization_barrier(jnp.mean(split * split, axis=-1, keepdims=True)) + EPSILON)
    return split.reshape(rows, width)

def project(state_in, member_noise, norm_gain, weight_query, weight_key, weight_value):
    member_rows, tokens, width = state_in.shape
    mixed = state_in + member_noise.astype(jnp.float32)
    normed = (mixed * lax.rsqrt(lax.optimization_barrier(jnp.mean(mixed * mixed, axis=-1, keepdims=True)) + EPSILON) * norm_gain).astype(jnp.bfloat16)
    flat = normed.reshape(member_rows * tokens, width)
    query = normalize_heads(jnp.dot(flat, weight_query, preferred_element_type=jnp.float32)).astype(jnp.bfloat16)
    key = normalize_heads(jnp.dot(flat, weight_key, preferred_element_type=jnp.float32)).astype(jnp.bfloat16)
    value = jnp.dot(flat, weight_value, preferred_element_type=jnp.float32).astype(jnp.bfloat16)
    full_shape = (member_rows, tokens, width)
    return (query.reshape(full_shape), key.reshape(full_shape), value.reshape(full_shape))

def attend(query, keys, values, leading_realization, total):
    member_rows, queries, width = query.shape
    realization_number = keys.shape[1]
    depth = width // HEADS
    query_heads = query.reshape(member_rows, queries, HEADS, depth).astype(jnp.float32)
    key_heads = keys.reshape(member_rows, realization_number, HEADS, depth).astype(jnp.float32)
    value_heads = values.reshape(member_rows, realization_number, HEADS, depth).astype(jnp.float32)
    scores = jnp.einsum('mqhd,mkhd->mhqk', query_heads, key_heads) / jnp.sqrt(jnp.float32(depth))
    query_pos = leading_realization + lax.iota(jnp.int32, queries)
    key_pos = leading_realization - HALF + lax.iota(jnp.int32, realization_number)
    allowed = (key_pos[None, :] >= query_pos[:, None] - HALF) & (key_pos[None, :] < query_pos[:, None] + HALF)
    allowed = allowed & (key_pos[None, :] >= 0) & (key_pos[None, :] < total)
    raised = jnp.where(allowed[None, None], jnp.exp(scores), jnp.float32(0.0))
    probs = (raised / lax.optimization_barrier(jnp.sum(raised, axis=-1, keepdims=True))).astype(jnp.bfloat16)
    mixed = jnp.einsum('mhqk,mkhd->mqhd', probs.astype(jnp.float32), value_heads)
    return mixed.reshape(member_rows, queries, width).astype(jnp.bfloat16)

def windowed(query, key, value):
    member_rows, total, width = query.shape
    padding = ((0, 0), (HALF, HALF), (0, 0))
    key_pad = jnp.pad(key, padding)
    value_pad = jnp.pad(value, padding)

    def block(index):
        beginning_shift = index * TOK_DEV
        query_block = lax.dynamic_slice_in_dim(query, beginning_shift, TOK_DEV, 1)
        key_block = lax.dynamic_slice_in_dim(key_pad, beginning_shift, TOK_DEV + 2 * HALF, 1)
        value_block = lax.dynamic_slice_in_dim(value_pad, beginning_shift, TOK_DEV + 2 * HALF, 1)
        return attend(query_block, key_block, value_block, beginning_shift, total)
    stacked = lax.map(jax.checkpoint(block), jnp.arange(total // TOK_DEV, dtype=jnp.int32))
    return jnp.transpose(stacked, (1, 0, 2, 3)).reshape(member_rows, total, width)

def softened_magnitude(diff):
    return jnp.sqrt(diff * diff + SMOOTH)

def unbiased_ranked_score(realization_prediction, observed_grid, surface_extent, quantity_scoring_factor):
    realization_number = realization_prediction.shape[0]
    accuracy_part = softened_magnitude(realization_prediction[0] - observed_grid)
    for realization_position in range(1, realization_number):
        accuracy_part = accuracy_part + softened_magnitude(realization_prediction[realization_position] - observed_grid)
    dispersion_part = jnp.zeros_like(accuracy_part)
    for leading_realization in range(realization_number):
        for paired_realization in range(leading_realization + 1, realization_number):
            dispersion_part = dispersion_part + softened_magnitude(realization_prediction[leading_realization] - realization_prediction[paired_realization])
    score = accuracy_part / realization_number - dispersion_part / (realization_number * (realization_number - 1))
    return jnp.sum(quantity_scoring_factor[:, None] * surface_extent[None, :] * score)

def reference(members_in, member_noise, norm_gain, weight_query, weight_key, weight_value, weight_out, decoder_projection_weight, decoder_bias, observations, surface_extent_factor, quantity_scoring_factor, point_map):
    location_entry_position = jnp.arange(POINTS, dtype=jnp.int32) // SITES_EACH_PART * TOK_DEV + point_map

    def overall_scoring_amount(state, out_f, decoder_f):
        member_rows, tokens, width = state.shape
        query, key, value = project(state, member_noise, norm_gain, weight_query, weight_key, weight_value)
        attended = windowed(query, key, value)
        update = jnp.dot(attended.reshape(member_rows * tokens, width), out_f.astype(jnp.bfloat16), preferred_element_type=jnp.float32)
        residual_stream_state = (state + member_noise.astype(jnp.float32) + update.reshape(member_rows, tokens, width)).astype(jnp.bfloat16)
        mapping_array = jnp.einsum('vc,mtc->mvt', decoder_f.astype(jnp.bfloat16).astype(jnp.float32), residual_stream_state.astype(jnp.float32))
        mapping_array = mapping_array + decoder_bias[None, :, None]
        realization_prediction = jnp.take(mapping_array, location_entry_position, axis=2)

        def block(index):
            beginning_shift = index * SITES_EACH_PART
            return unbiased_ranked_score(lax.dynamic_slice_in_dim(realization_prediction, beginning_shift, SITES_EACH_PART, 2), lax.dynamic_slice_in_dim(observations, beginning_shift, SITES_EACH_PART, 1), lax.dynamic_slice_in_dim(surface_extent_factor, beginning_shift, SITES_EACH_PART, 0), quantity_scoring_factor)
        parts = lax.map(jax.checkpoint(block), jnp.arange(POINTS // SITES_EACH_PART, dtype=jnp.int32))
        return jnp.sum(parts)
    total, pull = jax.vjp(overall_scoring_amount, members_in.astype(jnp.float32), weight_out.astype(jnp.float32), decoder_projection_weight.astype(jnp.float32))
    grad_state, grad_out, grad_decoder = pull(jnp.ones((), jnp.float32))
    mean_scoring = total / (VARS * POINTS)
    return (mean_scoring, grad_state.astype(jnp.bfloat16), grad_out, grad_decoder)
```

```python
import jax
import jax.numpy as jnp
from jax import lax
from jax.sharding import Mesh, PartitionSpec as P

HEADS = 16
HALF = 128
TOK = ("z_lo", "x", "y", "core")
TOK_SHAPE = (2, 4, 4, 2)
TOKENS_AXIS = 64


EPSILON = 1e-06
SMOOTH = 0.01


def extended_2(block, sides, width):
    for axis, dim in sides:
        count = TOKENS_AXIS
        forward = [(i, i + 1) for i in range(count - 1)]
        backward = [(target, source) for source, target in forward]
        low = lax.ppermute(
            lax.slice_in_dim(block, block.shape[dim] - width, None, axis=dim), axis, forward
        )
        high = lax.ppermute(lax.slice_in_dim(block, 0, width, axis=dim), axis, backward)
        block = jnp.concatenate([low, block, high], axis=dim)
    return block


def from_behind(block, axis, distance):
    devices = range(TOKENS_AXIS)
    route = [(i - distance, i) for i in devices if i - distance in devices]
    return lax.ppermute(block, axis, route)


def normalize_heads(flat):
    rows, width = flat.shape
    split = flat.reshape(rows, HEADS, width // HEADS)
    split = split * lax.rsqrt(jnp.mean(split * split, axis=-1, keepdims=True) + EPSILON)
    return split.reshape(rows, width)


def project(state_in, member_noise, norm_gain, weight_query, weight_key, weight_value):
    member_rows, tokens, width = state_in.shape
    mixed = state_in + member_noise.astype(jnp.float32)
    normed = (
        mixed * lax.rsqrt(jnp.mean(mixed * mixed, axis=-1, keepdims=True) + EPSILON) * norm_gain
    ).astype(jnp.bfloat16)
    flat = normed.reshape(member_rows * tokens, width)
    query = normalize_heads(jnp.dot(flat, weight_query, preferred_element_type=jnp.float32)).astype(
        jnp.bfloat16
    )
    key = normalize_heads(jnp.dot(flat, weight_key, preferred_element_type=jnp.float32)).astype(
        jnp.bfloat16
    )
    value = jnp.dot(flat, weight_value, preferred_element_type=jnp.float32).astype(jnp.bfloat16)
    full_shape = (member_rows, tokens, width)
    return (query.reshape(full_shape), key.reshape(full_shape), value.reshape(full_shape))


def attend(query, keys, values, leading_realization, total):
    member_rows, queries, width = query.shape
    realization_number = keys.shape[1]
    depth = width // HEADS
    query_heads = query.reshape(member_rows, queries, HEADS, depth)
    key_heads = keys.reshape(member_rows, realization_number, HEADS, depth)
    value_heads = values.reshape(member_rows, realization_number, HEADS, depth)
    scores = jnp.einsum(
        "mqhd,mkhd->mhqk", query_heads, key_heads, preferred_element_type=jnp.float32
    ) / jnp.sqrt(jnp.float32(depth))
    query_pos = leading_realization + lax.iota(jnp.int32, queries)
    key_pos = leading_realization - HALF + lax.iota(jnp.int32, realization_number)
    allowed = (key_pos[None, :] >= query_pos[:, None] - HALF) & (
        key_pos[None, :] < query_pos[:, None] + HALF
    )
    allowed = allowed & (key_pos[None, :] >= 0) & (key_pos[None, :] < total)
    raised = jnp.where(allowed[None, None], jnp.exp(scores), jnp.float32(0.0))
    probs = (raised / jnp.sum(raised, axis=-1, keepdims=True)).astype(jnp.bfloat16)
    mixed = jnp.einsum("mhqk,mkhd->mqhd", probs, value_heads, preferred_element_type=jnp.float32)
    return mixed.reshape(member_rows, queries, width).astype(jnp.bfloat16)


def softened_magnitude(diff):
    return jnp.sqrt(diff * diff + SMOOTH)


def unbiased_ranked_score(
    realization_prediction, observed_grid, surface_extent, quantity_scoring_factor
):
    realization_number = realization_prediction.shape[0]
    accuracy_part = softened_magnitude(realization_prediction[0] - observed_grid)
    for realization_position in range(1, realization_number):
        accuracy_part = accuracy_part + softened_magnitude(
            realization_prediction[realization_position] - observed_grid
        )
    dispersion_part = jnp.zeros_like(accuracy_part)
    for leading_realization in range(realization_number):
        for paired_realization in range(leading_realization + 1, realization_number):
            dispersion_part = dispersion_part + softened_magnitude(
                realization_prediction[leading_realization]
                - realization_prediction[paired_realization]
            )
    score = accuracy_part / realization_number - dispersion_part / (
        realization_number * (realization_number - 1)
    )
    return jnp.sum(quantity_scoring_factor[:, None] * surface_extent[None, :] * score)


def reduce_outputs(product, decoder_piece, loss_piece):
    blocks = TOKENS_AXIS
    rows, width = product.shape
    dec_rows = -(-(decoder_piece.shape[0] + 1) // blocks) * blocks
    padded = jnp.zeros((dec_rows, width), jnp.float32)
    padded = padded.at[: decoder_piece.shape[0]].set(decoder_piece)
    padded = padded.at[decoder_piece.shape[0], 0].set(loss_piece)
    own = rows // blocks
    merged = jnp.concatenate(
        [
            product.reshape(TOK_SHAPE + (own, width)),
            padded.reshape(TOK_SHAPE + (dec_rows // blocks, width)),
        ],
        axis=4,
    )
    merged = jnp.transpose(merged, (3, 1, 2, 0, 4, 5)).reshape(-1, width)
    for axis in ("core", "x", "y", "z_lo"):
        merged = lax.psum_scatter(merged, axis, scatter_dimension=0, tiled=True)
    merged = lax.psum(merged, "member")
    grad_out = merged[:own]
    dec = merged[own:]
    for axis in ("core", "y", "x", "z_lo"):
        dec = lax.all_gather(dec, axis, axis=0, tiled=True)
    return grad_out, dec[: decoder_piece.shape[0]], dec[decoder_piece.shape[0], 0]


def shards(
    members_in,
    member_noise,
    norm_gain,
    weight_query,
    weight_key,
    weight_value,
    weight_out,
    decoder_projection_weight,
    decoder_bias,
    observations,
    surface_extent_factor,
    quantity_scoring_factor,
    point_map,
):
    member_rows, tokens, width = members_in.shape
    state = members_in.astype(jnp.float32)

    def front(state_in):
        return project(state_in, member_noise, norm_gain, weight_query, weight_key, weight_value)

    (query, key, value), front_pull = jax.vjp(front, state)
    stacked = jnp.stack([key, value])
    extended = extended_2(stacked, ((TOK, 2),), HALF)
    leading_realization = lax.axis_index(TOK) * tokens
    total = tokens * TOKENS_AXIS

    def middle(query_in, extended_in):
        return attend(query_in, extended_in[0], extended_in[1], leading_realization, total)

    attended, middle_pull = jax.vjp(middle, query, extended)
    flat_att = attended.reshape(member_rows * tokens, width)
    update = jnp.dot(flat_att, weight_out, preferred_element_type=jnp.float32).reshape(
        member_rows, tokens, width
    )
    residual_stream_state = (state + member_noise.astype(jnp.float32) + update).astype(jnp.bfloat16)

    def decode_tokens(residual_in, decoder_in):
        mapping_array = jnp.einsum(
            "vc,mtc->mvt",
            decoder_in.astype(jnp.bfloat16),
            residual_in,
            preferred_element_type=jnp.float32,
        )
        return mapping_array + decoder_bias[None, :, None]

    token_prediction, readout_slope_pulled = jax.vjp(
        decode_tokens, residual_stream_state, decoder_projection_weight.astype(jnp.float32)
    )
    location_places = point_map.shape[0]
    groups = lax.axis_size("member")
    local_shard = lax.axis_index("member")
    gathered_tokens = lax.all_gather(token_prediction, "member", axis=0, tiled=True)
    selector = (point_map[:, None] == lax.iota(jnp.int32, tokens)[None, :]).astype(jnp.float32)
    gathered_lines = jnp.einsum(
        "mvt,pt->mvp", gathered_tokens, selector, precision=lax.Precision.HIGHEST
    )

    def score_all(whole):
        return unbiased_ranked_score(
            whole, observations, surface_extent_factor, quantity_scoring_factor
        )

    full_loss, score_pull = jax.vjp(score_all, gathered_lines)
    (complete_gradient,) = score_pull(jnp.ones((), jnp.float32))
    point_slope = lax.dynamic_slice_in_dim(
        complete_gradient, local_shard * member_rows, member_rows, 0
    )
    prediction_slope = jnp.einsum(
        "mvp,pt->mvt", point_slope, selector, precision=lax.Precision.HIGHEST
    )
    partial_loss = full_loss / groups
    carried_slope, readout_piece_result = readout_slope_pulled(prediction_slope)
    flat_grad = carried_slope.reshape(member_rows * tokens, width)
    contract = (((0,), (0,)), ((), ()))
    product = lax.dot_general(flat_att, flat_grad, contract, preferred_element_type=jnp.float32)
    grad_out, grad_decoder, overall_scoring_amount = reduce_outputs(
        product, readout_piece_result, partial_loss
    )
    mean_scoring = overall_scoring_amount / (
        token_prediction.shape[1] * location_places * TOKENS_AXIS
    )
    grad_attended = (
        jnp.dot(flat_grad, weight_out.T, preferred_element_type=jnp.float32)
        .astype(jnp.bfloat16)
        .reshape(member_rows, tokens, width)
    )
    grad_query, grad_extended = middle_pull(grad_attended)
    lower_rim = grad_extended[:, :, :HALF]
    upper_rim = grad_extended[:, :, tokens + HALF :]
    inner = grad_extended[:, :, HALF : tokens + HALF].astype(jnp.float32)
    from_next = from_behind(lower_rim, TOK, -1)
    from_prev = from_behind(upper_rim, TOK, 1)
    inner = inner.at[:, :, tokens - HALF :].add(from_next.astype(jnp.float32))
    inner = inner.at[:, :, :HALF].add(from_prev.astype(jnp.float32))
    (grad_front,) = front_pull(
        (grad_query, inner[0].astype(jnp.bfloat16), inner[1].astype(jnp.bfloat16))
    )
    grad_members = (grad_front + carried_slope.astype(jnp.float32)).astype(jnp.bfloat16)
    return (mean_scoring, grad_members, grad_out, grad_decoder)


def solution(mesh):
    assert mesh.shape["token"] == TOKENS_AXIS
    split = Mesh(
        mesh.devices.reshape((mesh.shape["member"],) + TOK_SHAPE), ("member",) + TOK
    )
    return jax.shard_map(
        shards,
        mesh=split,
        in_specs=(
            P("member", TOK, None),
            P("member", TOK, None),
            P(),
            P(),
            P(),
            P(),
            P(),
            P(),
            P(),
            P(None, TOK),
            P(TOK),
            P(),
            P(TOK),
        ),
        out_specs=(P(), P("member", TOK, None), P(TOK, None), P()),
        check_vma=False,
    )
```

```python
import jax
import jax.numpy as jnp
from jax import lax
from jax.sharding import Mesh, PartitionSpec as P

HEADS = 16
HALF = 128
TOK = ("z_lo", "x", "y", "core")
TOK_SHAPE = (2, 4, 4, 2)
TOKENS_AXIS = 64
MEMBER_AXIS = 4


EPSILON = 1e-06
SMOOTH = 0.01


def extended_2(block, sides, width):
    for axis, dim in sides:
        count = TOKENS_AXIS
        forward = [(i, i + 1) for i in range(count - 1)]
        backward = [(target, source) for source, target in forward]
        low = lax.ppermute(
            lax.slice_in_dim(block, block.shape[dim] - width, None, axis=dim), axis, forward
        )
        high = lax.ppermute(lax.slice_in_dim(block, 0, width, axis=dim), axis, backward)
        block = jnp.concatenate([low, block, high], axis=dim)
    return block


def from_behind(block, axis, distance):
    devices = range(TOKENS_AXIS)
    route = [(i - distance, i) for i in devices if i - distance in devices]
    return lax.ppermute(block, axis, route)


def normalize_heads(flat):
    rows, width = flat.shape
    split = flat.reshape(rows, HEADS, width // HEADS)
    split = split * lax.rsqrt(jnp.mean(split * split, axis=-1, keepdims=True) + EPSILON)
    return split.reshape(rows, width)


def project(state_in, member_noise, norm_gain, weight_query, weight_key, weight_value):
    member_rows, tokens, width = state_in.shape
    mixed = state_in + member_noise.astype(jnp.float32)
    normed = (
        mixed * lax.rsqrt(jnp.mean(mixed * mixed, axis=-1, keepdims=True) + EPSILON) * norm_gain
    ).astype(jnp.bfloat16)
    flat = normed.reshape(member_rows * tokens, width)
    query = normalize_heads(jnp.dot(flat, weight_query, preferred_element_type=jnp.float32)).astype(
        jnp.bfloat16
    )
    key = normalize_heads(jnp.dot(flat, weight_key, preferred_element_type=jnp.float32)).astype(
        jnp.bfloat16
    )
    value = jnp.dot(flat, weight_value, preferred_element_type=jnp.float32).astype(jnp.bfloat16)
    full_shape = (member_rows, tokens, width)
    return (query.reshape(full_shape), key.reshape(full_shape), value.reshape(full_shape))


def attend(query, keys, values, leading_realization, total):
    member_rows, queries, width = query.shape
    realization_number = keys.shape[1]
    depth = width // HEADS
    query_heads = query.reshape(member_rows, queries, HEADS, depth)
    key_heads = keys.reshape(member_rows, realization_number, HEADS, depth)
    value_heads = values.reshape(member_rows, realization_number, HEADS, depth)
    scores = jnp.einsum(
        "mqhd,mkhd->mhqk", query_heads, key_heads, preferred_element_type=jnp.float32
    ) / jnp.sqrt(jnp.float32(depth))
    query_pos = leading_realization + lax.iota(jnp.int32, queries)
    key_pos = leading_realization - HALF + lax.iota(jnp.int32, realization_number)
    allowed = (key_pos[None, :] >= query_pos[:, None] - HALF) & (
        key_pos[None, :] < query_pos[:, None] + HALF
    )
    allowed = allowed & (key_pos[None, :] >= 0) & (key_pos[None, :] < total)
    raised = jnp.where(allowed[None, None], jnp.exp(scores), jnp.float32(0.0))
    probs = (raised / jnp.sum(raised, axis=-1, keepdims=True)).astype(jnp.bfloat16)
    mixed = jnp.einsum("mhqk,mkhd->mqhd", probs, value_heads, preferred_element_type=jnp.float32)
    return mixed.reshape(member_rows, queries, width).astype(jnp.bfloat16)


def softened_magnitude(diff):
    return jnp.sqrt(diff * diff + SMOOTH)


def unbiased_ranked_score(
    realization_prediction, observed_grid, surface_extent, quantity_scoring_factor
):
    realization_number = realization_prediction.shape[0]
    accuracy_part = softened_magnitude(realization_prediction[0] - observed_grid)
    for realization_position in range(1, realization_number):
        accuracy_part = accuracy_part + softened_magnitude(
            realization_prediction[realization_position] - observed_grid
        )
    dispersion_part = jnp.zeros_like(accuracy_part)
    for leading_realization in range(realization_number):
        for paired_realization in range(leading_realization + 1, realization_number):
            dispersion_part = dispersion_part + softened_magnitude(
                realization_prediction[leading_realization]
                - realization_prediction[paired_realization]
            )
    score = accuracy_part / realization_number - dispersion_part / (
        realization_number * (realization_number - 1)
    )
    return jnp.sum(quantity_scoring_factor[:, None] * surface_extent[None, :] * score)


def doubling_sum(block, axis, count):
    distance = 1
    while distance < count:
        route = [(i, i ^ distance) for i in range(count)]
        block = block + lax.ppermute(block, axis, route)
        distance *= 2
    return block


def reduce_product(product):
    blocks = TOKENS_AXIS
    rows, width = product.shape
    own = rows // blocks
    merged = product.reshape(TOK_SHAPE + (own, width))
    merged = jnp.transpose(merged, (3, 1, 2, 0, 4, 5)).reshape(-1, width)
    for axis in ("core", "x", "y", "z_lo"):
        merged = lax.psum_scatter(merged, axis, scatter_dimension=0, tiled=True)
    return doubling_sum(merged, "member", MEMBER_AXIS)


def reduce_decoder(decoder_piece, loss_piece):
    rows, width = decoder_piece.shape
    padded = jnp.concatenate(
        [decoder_piece, jnp.zeros((1, width), jnp.float32).at[0, 0].set(loss_piece)], axis=0
    )
    padded = doubling_sum(padded, TOK, TOKENS_AXIS)
    padded = doubling_sum(padded, "member", MEMBER_AXIS)
    return padded[:rows], padded[rows, 0]


def shards(
    members_in,
    member_noise,
    norm_gain,
    weight_query,
    weight_key,
    weight_value,
    weight_out,
    decoder_projection_weight,
    decoder_bias,
    observations,
    surface_extent_factor,
    quantity_scoring_factor,
    point_map,
):
    member_rows, tokens, width = members_in.shape
    state = members_in.astype(jnp.float32)

    def front(state_in):
        return project(state_in, member_noise, norm_gain, weight_query, weight_key, weight_value)

    (query, key, value), front_pull = jax.vjp(front, state)
    stacked = jnp.stack([key, value])
    extended = extended_2(stacked, ((TOK, 2),), HALF)
    leading_realization = lax.axis_index(TOK) * tokens
    total = tokens * TOKENS_AXIS

    def middle(query_in, extended_in):
        return attend(query_in, extended_in[0], extended_in[1], leading_realization, total)

    attended, middle_pull = jax.vjp(middle, query, extended)
    flat_att = attended.reshape(member_rows * tokens, width)
    update = jnp.dot(flat_att, weight_out, preferred_element_type=jnp.float32).reshape(
        member_rows, tokens, width
    )
    residual_stream_state = (state + member_noise.astype(jnp.float32) + update).astype(jnp.bfloat16)

    def decode_tokens(residual_in, decoder_in):
        mapping_array = jnp.einsum(
            "vc,mtc->mvt",
            decoder_in.astype(jnp.bfloat16),
            residual_in,
            preferred_element_type=jnp.float32,
        )
        return mapping_array + decoder_bias[None, :, None]

    token_prediction, readout_slope_pulled = jax.vjp(
        decode_tokens, residual_stream_state, decoder_projection_weight.astype(jnp.float32)
    )
    location_places = point_map.shape[0]
    groups = lax.axis_size("member")
    local_shard = lax.axis_index("member")
    gathered_tokens = lax.all_gather(token_prediction, "member", axis=0, tiled=True)
    selector = (point_map[:, None] == lax.iota(jnp.int32, tokens)[None, :]).astype(jnp.float32)
    gathered_lines = jnp.einsum(
        "mvt,pt->mvp", gathered_tokens, selector, precision=lax.Precision.HIGHEST
    )

    def score_all(whole):
        return unbiased_ranked_score(
            whole, observations, surface_extent_factor, quantity_scoring_factor
        )

    full_loss, score_pull = jax.vjp(score_all, gathered_lines)
    (complete_gradient,) = score_pull(jnp.ones((), jnp.float32))
    point_slope = lax.dynamic_slice_in_dim(
        complete_gradient, local_shard * member_rows, member_rows, 0
    )
    prediction_slope = jnp.einsum(
        "mvp,pt->mvt", point_slope, selector, precision=lax.Precision.HIGHEST
    )
    partial_loss = full_loss / groups
    carried_slope, readout_piece_result = readout_slope_pulled(prediction_slope)
    flat_grad = carried_slope.reshape(member_rows * tokens, width)
    contract = (((0,), (0,)), ((), ()))
    product = lax.dot_general(flat_att, flat_grad, contract, preferred_element_type=jnp.float32)
    grad_decoder, overall_scoring_amount = reduce_decoder(readout_piece_result, partial_loss)
    grad_out = reduce_product(product)
    mean_scoring = overall_scoring_amount / (
        token_prediction.shape[1] * location_places * TOKENS_AXIS
    )
    grad_attended = (
        jnp.dot(flat_grad, weight_out.T, preferred_element_type=jnp.float32)
        .astype(jnp.bfloat16)
        .reshape(member_rows, tokens, width)
    )
    grad_query, grad_extended = middle_pull(grad_attended)
    lower_rim = grad_extended[:, :, :HALF]
    upper_rim = grad_extended[:, :, tokens + HALF :]
    inner = grad_extended[:, :, HALF : tokens + HALF].astype(jnp.float32)
    from_next = from_behind(lower_rim, TOK, -1)
    from_prev = from_behind(upper_rim, TOK, 1)
    inner = inner.at[:, :, tokens - HALF :].add(from_next.astype(jnp.float32))
    inner = inner.at[:, :, :HALF].add(from_prev.astype(jnp.float32))
    (grad_front,) = front_pull(
        (grad_query, inner[0].astype(jnp.bfloat16), inner[1].astype(jnp.bfloat16))
    )
    grad_members = (grad_front + carried_slope.astype(jnp.float32)).astype(jnp.bfloat16)
    return (mean_scoring, grad_members, grad_out, grad_decoder)


def solution(mesh):
    assert mesh.shape["token"] == TOKENS_AXIS
    assert mesh.shape["member"] == MEMBER_AXIS
    split = Mesh(
        mesh.devices.reshape((mesh.shape["member"],) + TOK_SHAPE), ("member",) + TOK
    )
    return jax.shard_map(
        shards,
        mesh=split,
        in_specs=(
            P("member", TOK, None),
            P("member", TOK, None),
            P(),
            P(),
            P(),
            P(),
            P(),
            P(),
            P(),
            P(None, TOK),
            P(TOK),
            P(),
            P(TOK),
        ),
        out_specs=(P(), P("member", TOK, None), P(TOK, None), P()),
        check_vma=False,
    )
```

```python
import jax
import jax.numpy as jnp
from jax import lax
from jax.sharding import Mesh, PartitionSpec as P

HEADS = 16
HALF = 128
TOK = ("z_lo", "x", "y", "core")
TOK_SHAPE = (2, 4, 4, 2)
TOKENS_AXIS = 64
MEMBER_AXIS = 4


EPSILON = 1e-06
SMOOTH = 0.01


def extended_2(block, sides, width):
    for axis, dim in sides:
        count = TOKENS_AXIS
        forward = [(i, i + 1) for i in range(count - 1)]
        backward = [(target, source) for source, target in forward]
        low = lax.ppermute(
            lax.slice_in_dim(block, block.shape[dim] - width, None, axis=dim), axis, forward
        )
        high = lax.ppermute(lax.slice_in_dim(block, 0, width, axis=dim), axis, backward)
        block = jnp.concatenate([low, block, high], axis=dim)
    return block


def from_behind(block, axis, distance):
    devices = range(TOKENS_AXIS)
    route = [(i - distance, i) for i in devices if i - distance in devices]
    return lax.ppermute(block, axis, route)


def normalize_heads(flat):
    rows, width = flat.shape
    split = flat.reshape(rows, HEADS, width // HEADS)
    split = split * lax.rsqrt(jnp.mean(split * split, axis=-1, keepdims=True) + EPSILON)
    return split.reshape(rows, width)


def project(state_in, member_noise, norm_gain, weight_query, weight_key, weight_value):
    member_rows, tokens, width = state_in.shape
    mixed = state_in + member_noise.astype(jnp.float32)
    normed = (
        mixed * lax.rsqrt(jnp.mean(mixed * mixed, axis=-1, keepdims=True) + EPSILON) * norm_gain
    ).astype(jnp.bfloat16)
    flat = normed.reshape(member_rows * tokens, width)
    query = normalize_heads(jnp.dot(flat, weight_query, preferred_element_type=jnp.float32)).astype(
        jnp.bfloat16
    )
    key = normalize_heads(jnp.dot(flat, weight_key, preferred_element_type=jnp.float32)).astype(
        jnp.bfloat16
    )
    value = jnp.dot(flat, weight_value, preferred_element_type=jnp.float32).astype(jnp.bfloat16)
    full_shape = (member_rows, tokens, width)
    return (query.reshape(full_shape), key.reshape(full_shape), value.reshape(full_shape))


def attend(query, keys, values, leading_realization, total):
    member_rows, queries, width = query.shape
    realization_number = keys.shape[1]
    depth = width // HEADS
    query_heads = query.reshape(member_rows, queries, HEADS, depth)
    key_heads = keys.reshape(member_rows, realization_number, HEADS, depth)
    value_heads = values.reshape(member_rows, realization_number, HEADS, depth)
    scores = jnp.einsum(
        "mqhd,mkhd->mhqk", query_heads, key_heads, preferred_element_type=jnp.float32
    ) / jnp.sqrt(jnp.float32(depth))
    query_pos = leading_realization + lax.iota(jnp.int32, queries)
    key_pos = leading_realization - HALF + lax.iota(jnp.int32, realization_number)
    allowed = (key_pos[None, :] >= query_pos[:, None] - HALF) & (
        key_pos[None, :] < query_pos[:, None] + HALF
    )
    allowed = allowed & (key_pos[None, :] >= 0) & (key_pos[None, :] < total)
    raised = jnp.where(allowed[None, None], jnp.exp(scores), jnp.float32(0.0))
    probs = (raised / jnp.sum(raised, axis=-1, keepdims=True)).astype(jnp.bfloat16)
    mixed = jnp.einsum("mhqk,mkhd->mqhd", probs, value_heads, preferred_element_type=jnp.float32)
    return mixed.reshape(member_rows, queries, width).astype(jnp.bfloat16)


def softened_magnitude(diff):
    return jnp.sqrt(diff * diff + SMOOTH)


def unbiased_ranked_score(
    realization_prediction, observed_grid, surface_extent, quantity_scoring_factor
):
    realization_number = realization_prediction.shape[0]
    accuracy_part = softened_magnitude(realization_prediction[0] - observed_grid)
    for realization_position in range(1, realization_number):
        accuracy_part = accuracy_part + softened_magnitude(
            realization_prediction[realization_position] - observed_grid
        )
    dispersion_part = jnp.zeros_like(accuracy_part)
    for leading_realization in range(realization_number):
        for paired_realization in range(leading_realization + 1, realization_number):
            dispersion_part = dispersion_part + softened_magnitude(
                realization_prediction[leading_realization]
                - realization_prediction[paired_realization]
            )
    score = accuracy_part / realization_number - dispersion_part / (
        realization_number * (realization_number - 1)
    )
    return jnp.sum(quantity_scoring_factor[:, None] * surface_extent[None, :] * score)


def doubling_sum(block, axis, count):
    distance = 1
    while distance < count:
        route = [(i, i ^ distance) for i in range(count)]
        block = block + lax.ppermute(block, axis, route)
        distance *= 2
    return block


def reduce_product(flat_att, flat_grad):
    rows, width = flat_att.shape
    own = width // TOKENS_AXIS
    core = lax.axis_index("core")
    swap = [(0, 1), (1, 0)]
    other_att = lax.ppermute(flat_att, "core", swap)
    other_grad = lax.ppermute(flat_grad, "core", swap)
    pair_att = jnp.concatenate([flat_att, other_att], axis=0)
    pair_grad = jnp.concatenate([flat_grad, other_grad], axis=0)
    picked = lax.dynamic_index_in_dim(
        pair_att.reshape(2 * rows, TOKENS_AXIS // 2, 2, own), core, axis=2, keepdims=False
    ).reshape(2 * rows, width // 2)
    contract = (((0,), (0,)), ((), ()))
    merged = lax.dot_general(picked, pair_grad, contract, preferred_element_type=jnp.float32)
    merged = merged.reshape(TOK_SHAPE[:3] + (own, width))
    merged = jnp.transpose(merged, (1, 2, 0, 3, 4)).reshape(-1, width)
    for axis in ("x", "y", "z_lo"):
        merged = lax.psum_scatter(merged, axis, scatter_dimension=0, tiled=True)
    return doubling_sum(merged, "member", MEMBER_AXIS)


def reduce_decoder(decoder_piece, loss_piece):
    rows, width = decoder_piece.shape
    padded = jnp.concatenate(
        [decoder_piece, jnp.zeros((1, width), jnp.float32).at[0, 0].set(loss_piece)], axis=0
    )
    padded = doubling_sum(padded, TOK, TOKENS_AXIS)
    padded = doubling_sum(padded, "member", MEMBER_AXIS)
    return padded[:rows], padded[rows, 0]


def shards(
    members_in,
    member_noise,
    norm_gain,
    weight_query,
    weight_key,
    weight_value,
    weight_out,
    decoder_projection_weight,
    decoder_bias,
    observations,
    surface_extent_factor,
    quantity_scoring_factor,
    point_map,
):
    member_rows, tokens, width = members_in.shape
    state = members_in.astype(jnp.float32)

    def front(state_in):
        return project(state_in, member_noise, norm_gain, weight_query, weight_key, weight_value)

    (query, key, value), front_pull = jax.vjp(front, state)
    stacked = jnp.stack([key, value])
    extended = extended_2(stacked, ((TOK, 2),), HALF)
    leading_realization = lax.axis_index(TOK) * tokens
    total = tokens * TOKENS_AXIS

    def middle(query_in, extended_in):
        return attend(query_in, extended_in[0], extended_in[1], leading_realization, total)

    attended, middle_pull = jax.vjp(middle, query, extended)
    flat_att = attended.reshape(member_rows * tokens, width)
    update = jnp.dot(flat_att, weight_out, preferred_element_type=jnp.float32).reshape(
        member_rows, tokens, width
    )
    residual_stream_state = (state + member_noise.astype(jnp.float32) + update).astype(jnp.bfloat16)

    def decode_tokens(residual_in, decoder_in):
        mapping_array = jnp.einsum(
            "vc,mtc->mvt",
            decoder_in.astype(jnp.bfloat16),
            residual_in,
            preferred_element_type=jnp.float32,
        )
        return mapping_array + decoder_bias[None, :, None]

    token_prediction, readout_slope_pulled = jax.vjp(
        decode_tokens, residual_stream_state, decoder_projection_weight.astype(jnp.float32)
    )
    location_places = point_map.shape[0]
    groups = lax.axis_size("member")
    local_shard = lax.axis_index("member")
    gathered_tokens = lax.all_gather(token_prediction, "member", axis=0, tiled=True)
    selector = (point_map[:, None] == lax.iota(jnp.int32, tokens)[None, :]).astype(jnp.float32)
    gathered_lines = jnp.einsum(
        "mvt,pt->mvp", gathered_tokens, selector, precision=lax.Precision.HIGHEST
    )

    def score_all(whole):
        return unbiased_ranked_score(
            whole, observations, surface_extent_factor, quantity_scoring_factor
        )

    full_loss, score_pull = jax.vjp(score_all, gathered_lines)
    (complete_gradient,) = score_pull(jnp.ones((), jnp.float32))
    point_slope = lax.dynamic_slice_in_dim(
        complete_gradient, local_shard * member_rows, member_rows, 0
    )
    prediction_slope = jnp.einsum(
        "mvp,pt->mvt", point_slope, selector, precision=lax.Precision.HIGHEST
    )
    partial_loss = full_loss / groups
    carried_slope, readout_piece_result = readout_slope_pulled(prediction_slope)
    flat_grad = carried_slope.reshape(member_rows * tokens, width)
    grad_decoder, overall_scoring_amount = reduce_decoder(readout_piece_result, partial_loss)
    grad_out = reduce_product(flat_att, flat_grad)
    mean_scoring = overall_scoring_amount / (
        token_prediction.shape[1] * location_places * TOKENS_AXIS
    )
    grad_attended = (
        jnp.dot(flat_grad, weight_out.T, preferred_element_type=jnp.float32)
        .astype(jnp.bfloat16)
        .reshape(member_rows, tokens, width)
    )
    grad_query, grad_extended = middle_pull(grad_attended)
    lower_rim = grad_extended[:, :, :HALF]
    upper_rim = grad_extended[:, :, tokens + HALF :]
    inner = grad_extended[:, :, HALF : tokens + HALF].astype(jnp.float32)
    from_next = from_behind(lower_rim, TOK, -1)
    from_prev = from_behind(upper_rim, TOK, 1)
    inner = inner.at[:, :, tokens - HALF :].add(from_next.astype(jnp.float32))
    inner = inner.at[:, :, :HALF].add(from_prev.astype(jnp.float32))
    (grad_front,) = front_pull(
        (grad_query, inner[0].astype(jnp.bfloat16), inner[1].astype(jnp.bfloat16))
    )
    grad_members = (grad_front + carried_slope.astype(jnp.float32)).astype(jnp.bfloat16)
    return (mean_scoring, grad_members, grad_out, grad_decoder)


def solution(mesh):
    assert mesh.shape["token"] == TOKENS_AXIS
    assert mesh.shape["member"] == MEMBER_AXIS
    split = Mesh(
        mesh.devices.reshape((mesh.shape["member"],) + TOK_SHAPE), ("member",) + TOK
    )
    return jax.shard_map(
        shards,
        mesh=split,
        in_specs=(
            P("member", TOK, None),
            P("member", TOK, None),
            P(),
            P(),
            P(),
            P(),
            P(),
            P(),
            P(),
            P(None, TOK),
            P(TOK),
            P(),
            P(TOK),
        ),
        out_specs=(P(), P("member", TOK, None), P(TOK, None), P()),
        check_vma=False,
    )
```

```python
import jax
import jax.numpy as jnp
from jax import lax
from jax.sharding import Mesh, PartitionSpec as P

HEADS = 16
HALF = 128
TOK = ("z_lo", "x", "y", "core")
TOK_SHAPE = (2, 4, 4, 2)
TOKENS_AXIS = 64
MEMBER_AXIS = 4


EPSILON = 1e-06
SMOOTH = 0.01


def extended_2(block, sides, width):
    for axis, dim in sides:
        count = TOKENS_AXIS
        forward = [(i, i + 1) for i in range(count - 1)]
        backward = [(target, source) for source, target in forward]
        low = lax.ppermute(
            lax.slice_in_dim(block, block.shape[dim] - width, None, axis=dim), axis, forward
        )
        high = lax.ppermute(lax.slice_in_dim(block, 0, width, axis=dim), axis, backward)
        block = jnp.concatenate([low, block, high], axis=dim)
    return block


def from_behind(block, axis, distance):
    devices = range(TOKENS_AXIS)
    route = [(i - distance, i) for i in devices if i - distance in devices]
    return lax.ppermute(block, axis, route)


def normalize_heads(flat):
    rows, width = flat.shape
    split = flat.reshape(rows, HEADS, width // HEADS)
    split = split * lax.rsqrt(jnp.mean(split * split, axis=-1, keepdims=True) + EPSILON)
    return split.reshape(rows, width)


def project(state_in, member_noise, norm_gain, weight_query, weight_key, weight_value):
    member_rows, tokens, width = state_in.shape
    mixed = state_in + member_noise.astype(jnp.float32)
    normed = (
        mixed * lax.rsqrt(jnp.mean(mixed * mixed, axis=-1, keepdims=True) + EPSILON) * norm_gain
    ).astype(jnp.bfloat16)
    flat = normed.reshape(member_rows * tokens, width)
    query = normalize_heads(jnp.dot(flat, weight_query, preferred_element_type=jnp.float32)).astype(
        jnp.bfloat16
    )
    key = normalize_heads(jnp.dot(flat, weight_key, preferred_element_type=jnp.float32)).astype(
        jnp.bfloat16
    )
    value = jnp.dot(flat, weight_value, preferred_element_type=jnp.float32).astype(jnp.bfloat16)
    full_shape = (member_rows, tokens, width)
    return (query.reshape(full_shape), key.reshape(full_shape), value.reshape(full_shape))


def attend(query, keys, values, leading_realization, total):
    member_rows, queries, width = query.shape
    realization_number = keys.shape[1]
    depth = width // HEADS
    query_heads = query.reshape(member_rows, queries, HEADS, depth)
    key_heads = keys.reshape(member_rows, realization_number, HEADS, depth)
    value_heads = values.reshape(member_rows, realization_number, HEADS, depth)
    scores = jnp.einsum(
        "mqhd,mkhd->mhqk", query_heads, key_heads, preferred_element_type=jnp.float32
    ) / jnp.sqrt(jnp.float32(depth))
    query_pos = leading_realization + lax.iota(jnp.int32, queries)
    key_pos = leading_realization - HALF + lax.iota(jnp.int32, realization_number)
    allowed = (key_pos[None, :] >= query_pos[:, None] - HALF) & (
        key_pos[None, :] < query_pos[:, None] + HALF
    )
    allowed = allowed & (key_pos[None, :] >= 0) & (key_pos[None, :] < total)
    raised = jnp.where(allowed[None, None], jnp.exp(scores), jnp.float32(0.0))
    probs = (raised / jnp.sum(raised, axis=-1, keepdims=True)).astype(jnp.bfloat16)
    mixed = jnp.einsum("mhqk,mkhd->mqhd", probs, value_heads, preferred_element_type=jnp.float32)
    return mixed.reshape(member_rows, queries, width).astype(jnp.bfloat16)


def softened_magnitude(diff):
    return jnp.sqrt(diff * diff + SMOOTH)


def unbiased_ranked_score(
    realization_prediction, observed_grid, surface_extent, quantity_scoring_factor
):
    realization_number = realization_prediction.shape[0]
    accuracy_part = softened_magnitude(realization_prediction[0] - observed_grid)
    for realization_position in range(1, realization_number):
        accuracy_part = accuracy_part + softened_magnitude(
            realization_prediction[realization_position] - observed_grid
        )
    dispersion_part = jnp.zeros_like(accuracy_part)
    for leading_realization in range(realization_number):
        for paired_realization in range(leading_realization + 1, realization_number):
            dispersion_part = dispersion_part + softened_magnitude(
                realization_prediction[leading_realization]
                - realization_prediction[paired_realization]
            )
    score = accuracy_part / realization_number - dispersion_part / (
        realization_number * (realization_number - 1)
    )
    return jnp.sum(quantity_scoring_factor[:, None] * surface_extent[None, :] * score)


def doubling_sum(block, axis, count):
    distance = 1
    while distance < count:
        route = [(i, i ^ distance) for i in range(count)]
        block = block + lax.ppermute(block, axis, route)
        distance *= 2
    return block


def reduce_all(crossed, decoder_piece, loss_piece, decoder_weight):
    width, variables = crossed.shape
    own = width // TOKENS_AXIS
    lanes = 256
    loss_column = jnp.zeros((width, 1), jnp.float32).at[0, 0].set(loss_piece)
    merged = jnp.concatenate(
        [
            crossed,
            decoder_piece.T,
            loss_column,
            jnp.zeros((width, lanes - 2 * variables - 1), jnp.float32),
        ],
        axis=1,
    )
    merged = merged.reshape(TOK_SHAPE + (own, lanes))
    merged = jnp.transpose(merged, (3, 1, 2, 0, 4, 5)).reshape(-1, lanes)
    for axis in ("core", "x", "y", "z_lo"):
        merged = lax.psum_scatter(merged, axis, scatter_dimension=0, tiled=True)
    merged = doubling_sum(merged, "member", MEMBER_AXIS)
    grad_out = jnp.dot(
        merged[:, :variables],
        decoder_weight.astype(jnp.float32),
        precision=lax.Precision.HIGHEST,
    )
    rest = merged[:, variables : variables + 128]
    for axis in ("core", "y", "x", "z_lo"):
        rest = lax.all_gather(rest, axis, axis=0, tiled=True)
    return grad_out, rest[:, :variables].T, rest[0, variables]


def shards(
    members_in,
    member_noise,
    norm_gain,
    weight_query,
    weight_key,
    weight_value,
    weight_out,
    decoder_projection_weight,
    decoder_bias,
    observations,
    surface_extent_factor,
    quantity_scoring_factor,
    point_map,
):
    member_rows, tokens, width = members_in.shape
    state = members_in.astype(jnp.float32)

    def front(state_in):
        return project(state_in, member_noise, norm_gain, weight_query, weight_key, weight_value)

    (query, key, value), front_pull = jax.vjp(front, state)
    stacked = jnp.stack([key, value])
    extended = extended_2(stacked, ((TOK, 2),), HALF)
    leading_realization = lax.axis_index(TOK) * tokens
    total = tokens * TOKENS_AXIS

    def middle(query_in, extended_in):
        return attend(query_in, extended_in[0], extended_in[1], leading_realization, total)

    attended, middle_pull = jax.vjp(middle, query, extended)
    flat_att = attended.reshape(member_rows * tokens, width)
    update = jnp.dot(flat_att, weight_out, preferred_element_type=jnp.float32).reshape(
        member_rows, tokens, width
    )
    residual_stream_state = (state + member_noise.astype(jnp.float32) + update).astype(jnp.bfloat16)

    def decode_tokens(residual_in, decoder_in):
        mapping_array = jnp.einsum(
            "vc,mtc->mvt",
            decoder_in.astype(jnp.bfloat16),
            residual_in,
            preferred_element_type=jnp.float32,
        )
        return mapping_array + decoder_bias[None, :, None]

    token_prediction, readout_slope_pulled = jax.vjp(
        decode_tokens, residual_stream_state, decoder_projection_weight.astype(jnp.float32)
    )
    location_places = point_map.shape[0]
    groups = lax.axis_size("member")
    local_shard = lax.axis_index("member")
    gathered_tokens = lax.all_gather(token_prediction, "member", axis=0, tiled=True)
    selector = (point_map[:, None] == lax.iota(jnp.int32, tokens)[None, :]).astype(jnp.float32)
    gathered_lines = jnp.einsum(
        "mvt,pt->mvp", gathered_tokens, selector, precision=lax.Precision.HIGHEST
    )

    def score_all(whole):
        return unbiased_ranked_score(
            whole, observations, surface_extent_factor, quantity_scoring_factor
        )

    full_loss, score_pull = jax.vjp(score_all, gathered_lines)
    (complete_gradient,) = score_pull(jnp.ones((), jnp.float32))
    point_slope = lax.dynamic_slice_in_dim(
        complete_gradient, local_shard * member_rows, member_rows, 0
    )
    prediction_slope = jnp.einsum(
        "mvp,pt->mvt", point_slope, selector, precision=lax.Precision.HIGHEST
    )
    partial_loss = full_loss / groups
    carried_slope, readout_piece_result = readout_slope_pulled(prediction_slope)
    flat_grad = carried_slope.reshape(member_rows * tokens, width)
    crossed = jnp.einsum(
        "mtc,mvt->cv",
        attended.astype(jnp.float32),
        prediction_slope,
        precision=lax.Precision.HIGHEST,
    )
    grad_out, grad_decoder, overall_scoring_amount = reduce_all(
        crossed, readout_piece_result, partial_loss, decoder_projection_weight
    )
    mean_scoring = overall_scoring_amount / (
        token_prediction.shape[1] * location_places * TOKENS_AXIS
    )
    grad_attended = (
        jnp.dot(flat_grad, weight_out.T, preferred_element_type=jnp.float32)
        .astype(jnp.bfloat16)
        .reshape(member_rows, tokens, width)
    )
    grad_query, grad_extended = middle_pull(grad_attended)
    lower_rim = grad_extended[:, :, :HALF]
    upper_rim = grad_extended[:, :, tokens + HALF :]
    inner = grad_extended[:, :, HALF : tokens + HALF].astype(jnp.float32)
    from_next = from_behind(lower_rim, TOK, -1)
    from_prev = from_behind(upper_rim, TOK, 1)
    inner = inner.at[:, :, tokens - HALF :].add(from_next.astype(jnp.float32))
    inner = inner.at[:, :, :HALF].add(from_prev.astype(jnp.float32))
    (grad_front,) = front_pull(
        (grad_query, inner[0].astype(jnp.bfloat16), inner[1].astype(jnp.bfloat16))
    )
    grad_members = (grad_front + carried_slope.astype(jnp.float32)).astype(jnp.bfloat16)
    return (mean_scoring, grad_members, grad_out, grad_decoder)


def solution(mesh):
    assert mesh.shape["token"] == TOKENS_AXIS
    assert mesh.shape["member"] == MEMBER_AXIS
    split = Mesh(
        mesh.devices.reshape((mesh.shape["member"],) + TOK_SHAPE), ("member",) + TOK
    )
    return jax.shard_map(
        shards,
        mesh=split,
        in_specs=(
            P("member", TOK, None),
            P("member", TOK, None),
            P(),
            P(),
            P(),
            P(),
            P(),
            P(),
            P(),
            P(None, TOK),
            P(TOK),
            P(),
            P(TOK),
        ),
        out_specs=(P(), P("member", TOK, None), P(TOK, None), P()),
        check_vma=False,
    )
```

```python
import jax
import jax.numpy as jnp
from jax import lax
from jax.sharding import Mesh, PartitionSpec as P


HEADS = 16
HALF = 128
TOK = ("z_lo", "x", "y", "core")
TOK_SHAPE = (2, 4, 4, 2)
TOKENS_AXIS = 64
MEMBER_AXIS = 4


EPSILON = 1e-06
SMOOTH = 0.01


def extended_2(block, sides, width):
    for axis, dim in sides:
        count = TOKENS_AXIS
        forward = [(i, i + 1) for i in range(count - 1)]
        backward = [(target, source) for source, target in forward]
        low = lax.ppermute(
            lax.slice_in_dim(block, block.shape[dim] - width, None, axis=dim), axis, forward
        )
        high = lax.ppermute(lax.slice_in_dim(block, 0, width, axis=dim), axis, backward)
        block = jnp.concatenate([low, block, high], axis=dim)
    return block


def from_behind(block, axis, distance):
    devices = range(TOKENS_AXIS)
    route = [(i - distance, i) for i in devices if i - distance in devices]
    return lax.ppermute(block, axis, route)


def normalize_heads(flat):
    rows, width = flat.shape
    split = flat.reshape(rows, HEADS, width // HEADS)
    split = split * lax.rsqrt(jnp.mean(split * split, axis=-1, keepdims=True) + EPSILON)
    return split.reshape(rows, width)


def project(state_in, member_noise, norm_gain, weight_query, weight_key, weight_value):
    member_rows, tokens, width = state_in.shape
    mixed = state_in + member_noise.astype(jnp.float32)
    normed = (
        mixed * lax.rsqrt(jnp.mean(mixed * mixed, axis=-1, keepdims=True) + EPSILON) * norm_gain
    ).astype(jnp.bfloat16)
    flat = normed.reshape(member_rows * tokens, width)
    query = normalize_heads(jnp.dot(flat, weight_query, preferred_element_type=jnp.float32)).astype(
        jnp.bfloat16
    )
    key = normalize_heads(jnp.dot(flat, weight_key, preferred_element_type=jnp.float32)).astype(
        jnp.bfloat16
    )
    value = jnp.dot(flat, weight_value, preferred_element_type=jnp.float32).astype(jnp.bfloat16)
    full_shape = (member_rows, tokens, width)
    return (query.reshape(full_shape), key.reshape(full_shape), value.reshape(full_shape))


def attend(query, keys, values, leading_realization, total):
    member_rows, queries, width = query.shape
    realization_number = keys.shape[1]
    depth = width // HEADS
    query_heads = query.reshape(member_rows, queries, HEADS, depth)
    key_heads = keys.reshape(member_rows, realization_number, HEADS, depth)
    value_heads = values.reshape(member_rows, realization_number, HEADS, depth)
    scores = jnp.einsum(
        "mqhd,mkhd->mhqk", query_heads, key_heads, preferred_element_type=jnp.float32
    ) / jnp.sqrt(jnp.float32(depth))
    query_pos = leading_realization + lax.iota(jnp.int32, queries)
    key_pos = leading_realization - HALF + lax.iota(jnp.int32, realization_number)
    allowed = (key_pos[None, :] >= query_pos[:, None] - HALF) & (
        key_pos[None, :] < query_pos[:, None] + HALF
    )
    allowed = allowed & (key_pos[None, :] >= 0) & (key_pos[None, :] < total)
    raised = jnp.where(allowed[None, None], jnp.exp(scores), jnp.float32(0.0))
    probs = (raised / jnp.sum(raised, axis=-1, keepdims=True)).astype(jnp.bfloat16)
    mixed = jnp.einsum("mhqk,mkhd->mqhd", probs, value_heads, preferred_element_type=jnp.float32)
    return mixed.reshape(member_rows, queries, width).astype(jnp.bfloat16)


def softened_magnitude(diff):
    return jnp.sqrt(diff * diff + SMOOTH)


def unbiased_ranked_score(
    realization_prediction, observed_grid, surface_extent, quantity_scoring_factor
):
    realization_number = realization_prediction.shape[0]
    accuracy_part = softened_magnitude(realization_prediction[0] - observed_grid)
    for realization_position in range(1, realization_number):
        accuracy_part = accuracy_part + softened_magnitude(
            realization_prediction[realization_position] - observed_grid
        )
    dispersion_part = jnp.zeros_like(accuracy_part)
    for leading_realization in range(realization_number):
        for paired_realization in range(leading_realization + 1, realization_number):
            dispersion_part = dispersion_part + softened_magnitude(
                realization_prediction[leading_realization]
                - realization_prediction[paired_realization]
            )
    score = accuracy_part / realization_number - dispersion_part / (
        realization_number * (realization_number - 1)
    )
    return jnp.sum(quantity_scoring_factor[:, None] * surface_extent[None, :] * score)


def doubling_sum(block, axis, count):
    distance = 1
    while distance < count:
        route = [(i, i ^ distance) for i in range(count)]
        block = block + lax.ppermute(block, axis, route)
        distance *= 2
    return block


def reduce_all(crossed, decoder_piece, loss_piece, decoder_weight):
    width, variables = crossed.shape
    own = width // TOKENS_AXIS
    lanes = 256
    loss_column = jnp.zeros((width, 1), jnp.float32).at[0, 0].set(loss_piece)
    merged = jnp.concatenate(
        [
            crossed,
            decoder_piece.T,
            loss_column,
            jnp.zeros((width, lanes - 2 * variables - 1), jnp.float32),
        ],
        axis=1,
    )
    merged = merged.reshape(TOK_SHAPE + (own, lanes))
    merged = jnp.transpose(merged, (1, 3, 2, 0, 4, 5)).reshape(-1, lanes)
    for axis in (("x", "core"), ("y", "z_lo")):
        merged = lax.psum_scatter(merged, axis, scatter_dimension=0, tiled=True)
    merged = doubling_sum(merged, "member", MEMBER_AXIS)
    grad_out = jnp.dot(
        merged[:, :variables],
        decoder_weight.astype(jnp.float32),
        precision=lax.Precision.HIGHEST,
    )
    rest = merged[:, variables : variables + 128]
    for axis in (("y", "z_lo"), ("x", "core")):
        rest = lax.all_gather(rest, axis, axis=0, tiled=True)
    rest = rest.reshape((TOK_SHAPE[1], TOK_SHAPE[3], TOK_SHAPE[2], TOK_SHAPE[0], own, 128))
    rest = jnp.transpose(rest, (3, 0, 2, 1, 4, 5)).reshape(width, 128)
    return grad_out, rest[:, :variables].T, rest[0, variables]


def shards(
    members_in,
    member_noise,
    norm_gain,
    weight_query,
    weight_key,
    weight_value,
    weight_out,
    decoder_projection_weight,
    decoder_bias,
    observations,
    surface_extent_factor,
    quantity_scoring_factor,
    point_map,
):
    member_rows, tokens, width = members_in.shape
    state = members_in.astype(jnp.float32)

    def front(state_in):
        return project(state_in, member_noise, norm_gain, weight_query, weight_key, weight_value)

    (query, key, value), front_pull = jax.vjp(front, state)
    stacked = jnp.stack([key, value])
    extended = extended_2(stacked, ((TOK, 2),), HALF)
    leading_realization = lax.axis_index(TOK) * tokens
    total = tokens * TOKENS_AXIS

    def middle(query_in, extended_in):
        return attend(query_in, extended_in[0], extended_in[1], leading_realization, total)

    attended, middle_pull = jax.vjp(middle, query, extended)
    flat_att = attended.reshape(member_rows * tokens, width)
    update = jnp.dot(flat_att, weight_out, preferred_element_type=jnp.float32).reshape(
        member_rows, tokens, width
    )
    residual_stream_state = (state + member_noise.astype(jnp.float32) + update).astype(jnp.bfloat16)

    def decode_tokens(residual_in, decoder_in):
        mapping_array = jnp.einsum(
            "vc,mtc->mvt",
            decoder_in.astype(jnp.bfloat16),
            residual_in,
            preferred_element_type=jnp.float32,
        )
        return mapping_array + decoder_bias[None, :, None]

    token_prediction, readout_slope_pulled = jax.vjp(
        decode_tokens, residual_stream_state, decoder_projection_weight.astype(jnp.float32)
    )
    location_places = point_map.shape[0]
    groups = lax.axis_size("member")
    local_shard = lax.axis_index("member")
    gathered_tokens = lax.all_gather(token_prediction, "member", axis=0, tiled=True)
    selector = (point_map[:, None] == lax.iota(jnp.int32, tokens)[None, :]).astype(jnp.float32)
    gathered_lines = jnp.einsum(
        "mvt,pt->mvp", gathered_tokens, selector, precision=lax.Precision.HIGHEST
    )

    def score_all(whole):
        return unbiased_ranked_score(
            whole, observations, surface_extent_factor, quantity_scoring_factor
        )

    full_loss, score_pull = jax.vjp(score_all, gathered_lines)
    (complete_gradient,) = score_pull(jnp.ones((), jnp.float32))
    point_slope = lax.dynamic_slice_in_dim(
        complete_gradient, local_shard * member_rows, member_rows, 0
    )
    prediction_slope = jnp.einsum(
        "mvp,pt->mvt", point_slope, selector, precision=lax.Precision.HIGHEST
    )
    partial_loss = full_loss / groups
    carried_slope, readout_piece_result = readout_slope_pulled(prediction_slope)
    flat_grad = carried_slope.reshape(member_rows * tokens, width)
    crossed = jnp.einsum(
        "mtc,mvt->cv",
        attended.astype(jnp.float32),
        prediction_slope,
        precision=lax.Precision.HIGHEST,
    )
    grad_out, grad_decoder, overall_scoring_amount = reduce_all(
        crossed, readout_piece_result, partial_loss, decoder_projection_weight
    )
    mean_scoring = overall_scoring_amount / (
        token_prediction.shape[1] * location_places * TOKENS_AXIS
    )
    grad_attended = (
        jnp.dot(flat_grad, weight_out.T, preferred_element_type=jnp.float32)
        .astype(jnp.bfloat16)
        .reshape(member_rows, tokens, width)
    )
    grad_query, grad_extended = middle_pull(grad_attended)
    lower_rim = grad_extended[:, :, :HALF]
    upper_rim = grad_extended[:, :, tokens + HALF :]
    inner = grad_extended[:, :, HALF : tokens + HALF].astype(jnp.float32)
    from_next = from_behind(lower_rim, TOK, -1)
    from_prev = from_behind(upper_rim, TOK, 1)
    inner = inner.at[:, :, tokens - HALF :].add(from_next.astype(jnp.float32))
    inner = inner.at[:, :, :HALF].add(from_prev.astype(jnp.float32))
    (grad_front,) = front_pull(
        (grad_query, inner[0].astype(jnp.bfloat16), inner[1].astype(jnp.bfloat16))
    )
    grad_members = (grad_front + carried_slope.astype(jnp.float32)).astype(jnp.bfloat16)
    return (mean_scoring, grad_members, grad_out, grad_decoder)


def solution(mesh):
    assert mesh.shape["token"] == TOKENS_AXIS
    assert mesh.shape["member"] == MEMBER_AXIS
    split = Mesh(
        mesh.devices.reshape((mesh.shape["member"],) + TOK_SHAPE), ("member",) + TOK
    )
    return jax.shard_map(
        shards,
        mesh=split,
        in_specs=(
            P("member", TOK, None),
            P("member", TOK, None),
            P(),
            P(),
            P(),
            P(),
            P(),
            P(),
            P(),
            P(None, TOK),
            P(TOK),
            P(),
            P(TOK),
        ),
        out_specs=(P(), P("member", TOK, None), P(TOK, None), P()),
        check_vma=False,
    )
```

```python
import jax
import jax.numpy as jnp
from jax import lax
from jax.sharding import Mesh, PartitionSpec as P


HEADS = 16
HALF = 128
TOK = ("z_lo", "x", "y", "core")
TOK_SHAPE = (2, 4, 4, 2)
TOKENS_AXIS = 64
MEMBER_AXIS = 4


EPSILON = 1e-06
SMOOTH = 0.01


def extended_2(block, sides, width):
    for axis, dim in sides:
        count = TOKENS_AXIS
        forward = [(i, i + 1) for i in range(count - 1)]
        backward = [(target, source) for source, target in forward]
        low = lax.ppermute(
            lax.slice_in_dim(block, block.shape[dim] - width, None, axis=dim), axis, forward
        )
        high = lax.ppermute(lax.slice_in_dim(block, 0, width, axis=dim), axis, backward)
        block = jnp.concatenate([low, block, high], axis=dim)
    return block


def from_behind(block, axis, distance):
    devices = range(TOKENS_AXIS)
    route = [(i - distance, i) for i in devices if i - distance in devices]
    return lax.ppermute(block, axis, route)


def normalize_heads(flat):
    rows, width = flat.shape
    split = flat.reshape(rows, HEADS, width // HEADS)
    split = split * lax.rsqrt(jnp.mean(split * split, axis=-1, keepdims=True) + EPSILON)
    return split.reshape(rows, width)


def project(state_in, member_noise, norm_gain, weight_query, weight_key, weight_value):
    member_rows, tokens, width = state_in.shape
    mixed = state_in + member_noise.astype(jnp.float32)
    normed = (
        mixed * lax.rsqrt(jnp.mean(mixed * mixed, axis=-1, keepdims=True) + EPSILON) * norm_gain
    ).astype(jnp.bfloat16)
    flat = normed.reshape(member_rows * tokens, width)
    query = normalize_heads(jnp.dot(flat, weight_query, preferred_element_type=jnp.float32)).astype(
        jnp.bfloat16
    )
    key = normalize_heads(jnp.dot(flat, weight_key, preferred_element_type=jnp.float32)).astype(
        jnp.bfloat16
    )
    value = jnp.dot(flat, weight_value, preferred_element_type=jnp.float32).astype(jnp.bfloat16)
    full_shape = (member_rows, tokens, width)
    return (query.reshape(full_shape), key.reshape(full_shape), value.reshape(full_shape))


def attend(query, keys, values, leading_realization, total):
    member_rows, queries, width = query.shape
    realization_number = keys.shape[1]
    depth = width // HEADS
    query_heads = query.reshape(member_rows, queries, HEADS, depth)
    key_heads = keys.reshape(member_rows, realization_number, HEADS, depth)
    value_heads = values.reshape(member_rows, realization_number, HEADS, depth)
    scores = jnp.einsum(
        "mqhd,mkhd->mhqk", query_heads, key_heads, preferred_element_type=jnp.float32
    ) / jnp.sqrt(jnp.float32(depth))
    query_pos = leading_realization + lax.iota(jnp.int32, queries)
    key_pos = leading_realization - HALF + lax.iota(jnp.int32, realization_number)
    allowed = (key_pos[None, :] >= query_pos[:, None] - HALF) & (
        key_pos[None, :] < query_pos[:, None] + HALF
    )
    allowed = allowed & (key_pos[None, :] >= 0) & (key_pos[None, :] < total)
    raised = jnp.where(allowed[None, None], jnp.exp(scores), jnp.float32(0.0))
    probs = (raised / jnp.sum(raised, axis=-1, keepdims=True)).astype(jnp.bfloat16)
    mixed = jnp.einsum("mhqk,mkhd->mqhd", probs, value_heads, preferred_element_type=jnp.float32)
    return mixed.reshape(member_rows, queries, width).astype(jnp.bfloat16)


def softened_magnitude(diff):
    return jnp.sqrt(diff * diff + SMOOTH)


def unbiased_ranked_score(
    realization_prediction, observed_grid, surface_extent, quantity_scoring_factor
):
    realization_number = realization_prediction.shape[0]
    accuracy_part = softened_magnitude(realization_prediction[0] - observed_grid)
    for realization_position in range(1, realization_number):
        accuracy_part = accuracy_part + softened_magnitude(
            realization_prediction[realization_position] - observed_grid
        )
    dispersion_part = jnp.zeros_like(accuracy_part)
    for leading_realization in range(realization_number):
        for paired_realization in range(leading_realization + 1, realization_number):
            dispersion_part = dispersion_part + softened_magnitude(
                realization_prediction[leading_realization]
                - realization_prediction[paired_realization]
            )
    score = accuracy_part / realization_number - dispersion_part / (
        realization_number * (realization_number - 1)
    )
    return jnp.sum(quantity_scoring_factor[:, None] * surface_extent[None, :] * score)


def doubling_sum(block, axis, count):
    distance = 1
    while distance < count:
        route = [(i, i ^ distance) for i in range(count)]
        block = block + lax.ppermute(block, axis, route)
        distance *= 2
    return block


def halving_scatter(block, axis, count):
    index = lax.axis_index(axis)
    distance = count // 2
    while distance >= 1:
        half = block.reshape((2, block.shape[0] // 2) + block.shape[1:])
        bit = (index // distance) % 2
        keep = lax.dynamic_index_in_dim(half, bit, 0, keepdims=False)
        send = lax.dynamic_index_in_dim(half, 1 - bit, 0, keepdims=False)
        route = [(i, i ^ distance) for i in range(count)]
        block = keep + lax.ppermute(send, axis, route)
        distance //= 2
    return block


def reduce_all(crossed, decoder_piece, loss_piece, decoder_weight):
    width, variables = crossed.shape
    own = width // TOKENS_AXIS
    lanes = 256
    loss_column = jnp.zeros((width, 1), jnp.float32).at[0, 0].set(loss_piece)
    merged = jnp.concatenate(
        [
            crossed,
            decoder_piece.T,
            loss_column,
            jnp.zeros((width, lanes - 2 * variables - 1), jnp.float32),
        ],
        axis=1,
    )
    merged = merged.reshape(TOK_SHAPE + (own, lanes))
    merged = jnp.transpose(merged, (3, 1, 2, 0, 4, 5)).reshape(-1, lanes)
    for axis in ("core", "x"):
        merged = lax.psum_scatter(merged, axis, scatter_dimension=0, tiled=True)
    merged = halving_scatter(merged, "y", TOK_SHAPE[2])
    merged = halving_scatter(merged, "z_lo", TOK_SHAPE[0])
    merged = doubling_sum(merged, "member", MEMBER_AXIS)
    grad_out = jnp.dot(
        merged[:, :variables],
        decoder_weight.astype(jnp.float32),
        precision=lax.Precision.HIGHEST,
    )
    rest = merged[:, variables : variables + 128]
    for axis in ("core", "y", "x", "z_lo"):
        rest = lax.all_gather(rest, axis, axis=0, tiled=True)
    return grad_out, rest[:, :variables].T, rest[0, variables]


def shards(
    members_in,
    member_noise,
    norm_gain,
    weight_query,
    weight_key,
    weight_value,
    weight_out,
    decoder_projection_weight,
    decoder_bias,
    observations,
    surface_extent_factor,
    quantity_scoring_factor,
    point_map,
):
    member_rows, tokens, width = members_in.shape
    state = members_in.astype(jnp.float32)

    def front(state_in):
        return project(state_in, member_noise, norm_gain, weight_query, weight_key, weight_value)

    (query, key, value), front_pull = jax.vjp(front, state)
    stacked = jnp.stack([key, value])
    extended = extended_2(stacked, ((TOK, 2),), HALF)
    leading_realization = lax.axis_index(TOK) * tokens
    total = tokens * TOKENS_AXIS

    def middle(query_in, extended_in):
        return attend(query_in, extended_in[0], extended_in[1], leading_realization, total)

    attended, middle_pull = jax.vjp(middle, query, extended)
    flat_att = attended.reshape(member_rows * tokens, width)
    update = jnp.dot(flat_att, weight_out, preferred_element_type=jnp.float32).reshape(
        member_rows, tokens, width
    )
    residual_stream_state = (state + member_noise.astype(jnp.float32) + update).astype(jnp.bfloat16)

    def decode_tokens(residual_in, decoder_in):
        mapping_array = jnp.einsum(
            "vc,mtc->mvt",
            decoder_in.astype(jnp.bfloat16),
            residual_in,
            preferred_element_type=jnp.float32,
        )
        return mapping_array + decoder_bias[None, :, None]

    token_prediction, readout_slope_pulled = jax.vjp(
        decode_tokens, residual_stream_state, decoder_projection_weight.astype(jnp.float32)
    )
    location_places = point_map.shape[0]
    groups = lax.axis_size("member")
    local_shard = lax.axis_index("member")
    gathered_tokens = lax.all_gather(token_prediction, "member", axis=0, tiled=True)
    selector = (point_map[:, None] == lax.iota(jnp.int32, tokens)[None, :]).astype(jnp.float32)
    gathered_lines = jnp.einsum(
        "mvt,pt->mvp", gathered_tokens, selector, precision=lax.Precision.HIGHEST
    )

    def score_all(whole):
        return unbiased_ranked_score(
            whole, observations, surface_extent_factor, quantity_scoring_factor
        )

    full_loss, score_pull = jax.vjp(score_all, gathered_lines)
    (complete_gradient,) = score_pull(jnp.ones((), jnp.float32))
    point_slope = lax.dynamic_slice_in_dim(
        complete_gradient, local_shard * member_rows, member_rows, 0
    )
    prediction_slope = jnp.einsum(
        "mvp,pt->mvt", point_slope, selector, precision=lax.Precision.HIGHEST
    )
    partial_loss = full_loss / groups
    carried_slope, readout_piece_result = readout_slope_pulled(prediction_slope)
    flat_grad = carried_slope.reshape(member_rows * tokens, width)
    crossed = jnp.einsum(
        "mtc,mvt->cv",
        attended.astype(jnp.float32),
        prediction_slope,
        precision=lax.Precision.HIGHEST,
    )
    grad_out, grad_decoder, overall_scoring_amount = reduce_all(
        crossed, readout_piece_result, partial_loss, decoder_projection_weight
    )
    mean_scoring = overall_scoring_amount / (
        token_prediction.shape[1] * location_places * TOKENS_AXIS
    )
    grad_attended = (
        jnp.dot(flat_grad, weight_out.T, preferred_element_type=jnp.float32)
        .astype(jnp.bfloat16)
        .reshape(member_rows, tokens, width)
    )
    grad_query, grad_extended = middle_pull(grad_attended)
    lower_rim = grad_extended[:, :, :HALF]
    upper_rim = grad_extended[:, :, tokens + HALF :]
    inner = grad_extended[:, :, HALF : tokens + HALF].astype(jnp.float32)
    from_next = from_behind(lower_rim, TOK, -1)
    from_prev = from_behind(upper_rim, TOK, 1)
    inner = inner.at[:, :, tokens - HALF :].add(from_next.astype(jnp.float32))
    inner = inner.at[:, :, :HALF].add(from_prev.astype(jnp.float32))
    (grad_front,) = front_pull(
        (grad_query, inner[0].astype(jnp.bfloat16), inner[1].astype(jnp.bfloat16))
    )
    grad_members = (grad_front + carried_slope.astype(jnp.float32)).astype(jnp.bfloat16)
    return (mean_scoring, grad_members, grad_out, grad_decoder)


def solution(mesh):
    assert mesh.shape["token"] == TOKENS_AXIS
    assert mesh.shape["member"] == MEMBER_AXIS
    split = Mesh(
        mesh.devices.reshape((mesh.shape["member"],) + TOK_SHAPE), ("member",) + TOK
    )
    return jax.shard_map(
        shards,
        mesh=split,
        in_specs=(
            P("member", TOK, None),
            P("member", TOK, None),
            P(),
            P(),
            P(),
            P(),
            P(),
            P(),
            P(),
            P(None, TOK),
            P(TOK),
            P(),
            P(TOK),
        ),
        out_specs=(P(), P("member", TOK, None), P(TOK, None), P()),
        check_vma=False,
    )
```

```python
import jax
import jax.numpy as jnp
from jax import lax
from jax.sharding import Mesh, PartitionSpec as P


HEADS = 16
HALF = 128
TOK = ("z_lo", "x", "y", "core")
TOK_SHAPE = (2, 4, 4, 2)
TOKENS_AXIS = 64
MEMBER_AXIS = 4


EPSILON = 1e-06
SMOOTH = 0.01


def extended_2(block, sides, width):
    for axis, dim in sides:
        count = TOKENS_AXIS
        forward = [(i, i + 1) for i in range(count - 1)]
        backward = [(target, source) for source, target in forward]
        low = lax.ppermute(
            lax.slice_in_dim(block, block.shape[dim] - width, None, axis=dim), axis, forward
        )
        high = lax.ppermute(lax.slice_in_dim(block, 0, width, axis=dim), axis, backward)
        block = jnp.concatenate([low, block, high], axis=dim)
    return block


def from_behind(block, axis, distance):
    devices = range(TOKENS_AXIS)
    route = [(i - distance, i) for i in devices if i - distance in devices]
    return lax.ppermute(block, axis, route)


def normalize_heads(flat):
    rows, width = flat.shape
    split = flat.reshape(rows, HEADS, width // HEADS)
    split = split * lax.rsqrt(jnp.mean(split * split, axis=-1, keepdims=True) + EPSILON)
    return split.reshape(rows, width)


def project(state_in, member_noise, norm_gain, weight_query, weight_key, weight_value):
    member_rows, tokens, width = state_in.shape
    mixed = state_in + member_noise.astype(jnp.float32)
    normed = (
        mixed * lax.rsqrt(jnp.mean(mixed * mixed, axis=-1, keepdims=True) + EPSILON) * norm_gain
    ).astype(jnp.bfloat16)
    flat = normed.reshape(member_rows * tokens, width)
    query = normalize_heads(jnp.dot(flat, weight_query, preferred_element_type=jnp.float32)).astype(
        jnp.bfloat16
    )
    key = normalize_heads(jnp.dot(flat, weight_key, preferred_element_type=jnp.float32)).astype(
        jnp.bfloat16
    )
    value = jnp.dot(flat, weight_value, preferred_element_type=jnp.float32).astype(jnp.bfloat16)
    full_shape = (member_rows, tokens, width)
    return (query.reshape(full_shape), key.reshape(full_shape), value.reshape(full_shape))


def attend(query, keys, values, leading_realization, total):
    member_rows, queries, width = query.shape
    realization_number = keys.shape[1]
    depth = width // HEADS
    query_heads = query.reshape(member_rows, queries, HEADS, depth)
    key_heads = keys.reshape(member_rows, realization_number, HEADS, depth)
    value_heads = values.reshape(member_rows, realization_number, HEADS, depth)
    scores = jnp.einsum(
        "mqhd,mkhd->mhqk", query_heads, key_heads, preferred_element_type=jnp.float32
    ) / jnp.sqrt(jnp.float32(depth))
    query_pos = leading_realization + lax.iota(jnp.int32, queries)
    key_pos = leading_realization - HALF + lax.iota(jnp.int32, realization_number)
    allowed = (key_pos[None, :] >= query_pos[:, None] - HALF) & (
        key_pos[None, :] < query_pos[:, None] + HALF
    )
    allowed = allowed & (key_pos[None, :] >= 0) & (key_pos[None, :] < total)
    raised = jnp.where(allowed[None, None], jnp.exp(scores), jnp.float32(0.0))
    probs = (raised / jnp.sum(raised, axis=-1, keepdims=True)).astype(jnp.bfloat16)
    mixed = jnp.einsum("mhqk,mkhd->mqhd", probs, value_heads, preferred_element_type=jnp.float32)
    return mixed.reshape(member_rows, queries, width).astype(jnp.bfloat16)


def softened_magnitude(diff):
    return jnp.sqrt(diff * diff + SMOOTH)


def unbiased_ranked_score(
    realization_prediction, observed_grid, surface_extent, quantity_scoring_factor
):
    realization_number = realization_prediction.shape[0]
    accuracy_part = softened_magnitude(realization_prediction[0] - observed_grid)
    for realization_position in range(1, realization_number):
        accuracy_part = accuracy_part + softened_magnitude(
            realization_prediction[realization_position] - observed_grid
        )
    dispersion_part = jnp.zeros_like(accuracy_part)
    for leading_realization in range(realization_number):
        for paired_realization in range(leading_realization + 1, realization_number):
            dispersion_part = dispersion_part + softened_magnitude(
                realization_prediction[leading_realization]
                - realization_prediction[paired_realization]
            )
    score = accuracy_part / realization_number - dispersion_part / (
        realization_number * (realization_number - 1)
    )
    return jnp.sum(quantity_scoring_factor[:, None] * surface_extent[None, :] * score)


def doubling_sum(block, axis, count):
    distance = 1
    while distance < count:
        route = [(i, i ^ distance) for i in range(count)]
        block = block + lax.ppermute(block, axis, route)
        distance *= 2
    return block


def halving_scatter(block, axis, count):
    index = lax.axis_index(axis)
    distance = count // 2
    while distance >= 1:
        half = block.reshape((2, block.shape[0] // 2) + block.shape[1:])
        bit = (index // distance) % 2
        keep = lax.dynamic_index_in_dim(half, bit, 0, keepdims=False)
        send = lax.dynamic_index_in_dim(half, 1 - bit, 0, keepdims=False)
        route = [(i, i ^ distance) for i in range(count)]
        block = keep + lax.ppermute(send, axis, route)
        distance //= 2
    return block


def reduce_all(crossed, decoder_piece, loss_piece, decoder_weight):
    width, variables = crossed.shape
    own = width // TOKENS_AXIS
    lanes = 256
    loss_column = jnp.zeros((width, 1), jnp.float32).at[0, 0].set(loss_piece)
    merged = jnp.concatenate(
        [
            crossed,
            decoder_piece.T,
            loss_column,
            jnp.zeros((width, lanes - 2 * variables - 1), jnp.float32),
        ],
        axis=1,
    )
    merged = merged.reshape(TOK_SHAPE + (own, lanes))
    merged = jnp.transpose(merged, (3, 1, 2, 0, 4, 5)).reshape(-1, lanes)
    merged = lax.psum_scatter(merged, "core", scatter_dimension=0, tiled=True)
    merged = halving_scatter(merged, "x", TOK_SHAPE[1])
    merged = halving_scatter(merged, "y", TOK_SHAPE[2])
    merged = halving_scatter(merged, "z_lo", TOK_SHAPE[0])
    merged = doubling_sum(merged, "member", MEMBER_AXIS)
    grad_out = jnp.dot(
        merged[:, :variables],
        decoder_weight.astype(jnp.float32),
        precision=lax.Precision.HIGHEST,
    )
    rest = merged[:, variables : variables + 128]
    for axis in ("core", "y", "x", "z_lo"):
        rest = lax.all_gather(rest, axis, axis=0, tiled=True)
    return grad_out, rest[:, :variables].T, rest[0, variables]


def shards(
    members_in,
    member_noise,
    norm_gain,
    weight_query,
    weight_key,
    weight_value,
    weight_out,
    decoder_projection_weight,
    decoder_bias,
    observations,
    surface_extent_factor,
    quantity_scoring_factor,
    point_map,
):
    member_rows, tokens, width = members_in.shape
    state = members_in.astype(jnp.float32)

    def front(state_in):
        return project(state_in, member_noise, norm_gain, weight_query, weight_key, weight_value)

    (query, key, value), front_pull = jax.vjp(front, state)
    stacked = jnp.stack([key, value])
    extended = extended_2(stacked, ((TOK, 2),), HALF)
    leading_realization = lax.axis_index(TOK) * tokens
    total = tokens * TOKENS_AXIS

    def middle(query_in, extended_in):
        return attend(query_in, extended_in[0], extended_in[1], leading_realization, total)

    attended, middle_pull = jax.vjp(middle, query, extended)
    flat_att = attended.reshape(member_rows * tokens, width)
    update = jnp.dot(flat_att, weight_out, preferred_element_type=jnp.float32).reshape(
        member_rows, tokens, width
    )
    residual_stream_state = (state + member_noise.astype(jnp.float32) + update).astype(jnp.bfloat16)

    def decode_tokens(residual_in, decoder_in):
        mapping_array = jnp.einsum(
            "vc,mtc->mvt",
            decoder_in.astype(jnp.bfloat16),
            residual_in,
            preferred_element_type=jnp.float32,
        )
        return mapping_array + decoder_bias[None, :, None]

    token_prediction, readout_slope_pulled = jax.vjp(
        decode_tokens, residual_stream_state, decoder_projection_weight.astype(jnp.float32)
    )
    location_places = point_map.shape[0]
    groups = lax.axis_size("member")
    local_shard = lax.axis_index("member")
    gathered_tokens = lax.all_gather(token_prediction, "member", axis=0, tiled=True)
    selector = (point_map[:, None] == lax.iota(jnp.int32, tokens)[None, :]).astype(jnp.float32)
    gathered_lines = jnp.einsum(
        "mvt,pt->mvp", gathered_tokens, selector, precision=lax.Precision.HIGHEST
    )

    def score_all(whole):
        return unbiased_ranked_score(
            whole, observations, surface_extent_factor, quantity_scoring_factor
        )

    full_loss, score_pull = jax.vjp(score_all, gathered_lines)
    (complete_gradient,) = score_pull(jnp.ones((), jnp.float32))
    point_slope = lax.dynamic_slice_in_dim(
        complete_gradient, local_shard * member_rows, member_rows, 0
    )
    prediction_slope = jnp.einsum(
        "mvp,pt->mvt", point_slope, selector, precision=lax.Precision.HIGHEST
    )
    partial_loss = full_loss / groups
    carried_slope, readout_piece_result = readout_slope_pulled(prediction_slope)
    flat_grad = carried_slope.reshape(member_rows * tokens, width)
    crossed = jnp.einsum(
        "mtc,mvt->cv",
        attended.astype(jnp.float32),
        prediction_slope,
        precision=lax.Precision.HIGHEST,
    )
    grad_out, grad_decoder, overall_scoring_amount = reduce_all(
        crossed, readout_piece_result, partial_loss, decoder_projection_weight
    )
    mean_scoring = overall_scoring_amount / (
        token_prediction.shape[1] * location_places * TOKENS_AXIS
    )
    grad_attended = (
        jnp.dot(flat_grad, weight_out.T, preferred_element_type=jnp.float32)
        .astype(jnp.bfloat16)
        .reshape(member_rows, tokens, width)
    )
    grad_query, grad_extended = middle_pull(grad_attended)
    lower_rim = grad_extended[:, :, :HALF]
    upper_rim = grad_extended[:, :, tokens + HALF :]
    inner = grad_extended[:, :, HALF : tokens + HALF].astype(jnp.float32)
    from_next = from_behind(lower_rim, TOK, -1)
    from_prev = from_behind(upper_rim, TOK, 1)
    inner = inner.at[:, :, tokens - HALF :].add(from_next.astype(jnp.float32))
    inner = inner.at[:, :, :HALF].add(from_prev.astype(jnp.float32))
    (grad_front,) = front_pull(
        (grad_query, inner[0].astype(jnp.bfloat16), inner[1].astype(jnp.bfloat16))
    )
    grad_members = (grad_front + carried_slope.astype(jnp.float32)).astype(jnp.bfloat16)
    return (mean_scoring, grad_members, grad_out, grad_decoder)


def solution(mesh):
    assert mesh.shape["token"] == TOKENS_AXIS
    assert mesh.shape["member"] == MEMBER_AXIS
    split = Mesh(
        mesh.devices.reshape((mesh.shape["member"],) + TOK_SHAPE), ("member",) + TOK
    )
    return jax.shard_map(
        shards,
        mesh=split,
        in_specs=(
            P("member", TOK, None),
            P("member", TOK, None),
            P(),
            P(),
            P(),
            P(),
            P(),
            P(),
            P(),
            P(None, TOK),
            P(TOK),
            P(),
            P(TOK),
        ),
        out_specs=(P(), P("member", TOK, None), P(TOK, None), P()),
        check_vma=False,
    )
```

```python
import jax
import jax.numpy as jnp
from jax import lax
from jax.sharding import Mesh, PartitionSpec as P


HEADS = 16
HALF = 128
TOK = ("z_lo", "x", "y", "core")
TOK_SHAPE = (2, 4, 4, 2)
TOKENS_AXIS = 64
MEMBER_AXIS = 4


EPSILON = 1e-06
SMOOTH = 0.01


def extended_2(block, sides, width):
    for axis, dim in sides:
        count = TOKENS_AXIS
        forward = [(i, i + 1) for i in range(count - 1)]
        backward = [(target, source) for source, target in forward]
        low = lax.ppermute(
            lax.slice_in_dim(block, block.shape[dim] - width, None, axis=dim), axis, forward
        )
        high = lax.ppermute(lax.slice_in_dim(block, 0, width, axis=dim), axis, backward)
        block = jnp.concatenate([low, block, high], axis=dim)
    return block


def from_behind(block, axis, distance):
    devices = range(TOKENS_AXIS)
    route = [(i - distance, i) for i in devices if i - distance in devices]
    return lax.ppermute(block, axis, route)


def normalize_heads(flat):
    rows, width = flat.shape
    split = flat.reshape(rows, HEADS, width // HEADS)
    split = split * lax.rsqrt(jnp.mean(split * split, axis=-1, keepdims=True) + EPSILON)
    return split.reshape(rows, width)


def project(state_in, member_noise, norm_gain, weight_query, weight_key, weight_value):
    member_rows, tokens, width = state_in.shape
    mixed = state_in + member_noise.astype(jnp.float32)
    normed = (
        mixed * lax.rsqrt(jnp.mean(mixed * mixed, axis=-1, keepdims=True) + EPSILON) * norm_gain
    ).astype(jnp.bfloat16)
    flat = normed.reshape(member_rows * tokens, width)
    query = normalize_heads(jnp.dot(flat, weight_query, preferred_element_type=jnp.float32)).astype(
        jnp.bfloat16
    )
    key = normalize_heads(jnp.dot(flat, weight_key, preferred_element_type=jnp.float32)).astype(
        jnp.bfloat16
    )
    value = jnp.dot(flat, weight_value, preferred_element_type=jnp.float32).astype(jnp.bfloat16)
    full_shape = (member_rows, tokens, width)
    return (query.reshape(full_shape), key.reshape(full_shape), value.reshape(full_shape))


def attend(query, keys, values, leading_realization, total):
    member_rows, queries, width = query.shape
    realization_number = keys.shape[1]
    depth = width // HEADS
    query_heads = query.reshape(member_rows, queries, HEADS, depth)
    key_heads = keys.reshape(member_rows, realization_number, HEADS, depth)
    value_heads = values.reshape(member_rows, realization_number, HEADS, depth)
    scores = jnp.einsum(
        "mqhd,mkhd->mhqk", query_heads, key_heads, preferred_element_type=jnp.float32
    ) / jnp.sqrt(jnp.float32(depth))
    query_pos = leading_realization + lax.iota(jnp.int32, queries)
    key_pos = leading_realization - HALF + lax.iota(jnp.int32, realization_number)
    allowed = (key_pos[None, :] >= query_pos[:, None] - HALF) & (
        key_pos[None, :] < query_pos[:, None] + HALF
    )
    allowed = allowed & (key_pos[None, :] >= 0) & (key_pos[None, :] < total)
    raised = jnp.where(allowed[None, None], jnp.exp(scores), jnp.float32(0.0))
    probs = (raised / jnp.sum(raised, axis=-1, keepdims=True)).astype(jnp.bfloat16)
    mixed = jnp.einsum("mhqk,mkhd->mqhd", probs, value_heads, preferred_element_type=jnp.float32)
    return mixed.reshape(member_rows, queries, width).astype(jnp.bfloat16)


def softened_magnitude(diff):
    return jnp.sqrt(diff * diff + SMOOTH)


def unbiased_ranked_score(
    realization_prediction, observed_grid, surface_extent, quantity_scoring_factor
):
    realization_number = realization_prediction.shape[0]
    accuracy_part = softened_magnitude(realization_prediction[0] - observed_grid)
    for realization_position in range(1, realization_number):
        accuracy_part = accuracy_part + softened_magnitude(
            realization_prediction[realization_position] - observed_grid
        )
    dispersion_part = jnp.zeros_like(accuracy_part)
    for leading_realization in range(realization_number):
        for paired_realization in range(leading_realization + 1, realization_number):
            dispersion_part = dispersion_part + softened_magnitude(
                realization_prediction[leading_realization]
                - realization_prediction[paired_realization]
            )
    score = accuracy_part / realization_number - dispersion_part / (
        realization_number * (realization_number - 1)
    )
    return jnp.sum(quantity_scoring_factor[:, None] * surface_extent[None, :] * score)


def doubling_sum(block, axis, count):
    distance = 1
    while distance < count:
        route = [(i, i ^ distance) for i in range(count)]
        block = block + lax.ppermute(block, axis, route)
        distance *= 2
    return block


def halving_scatter(block, axis, count):
    index = lax.axis_index(axis)
    distance = count // 2
    while distance >= 1:
        half = block.reshape((2, block.shape[0] // 2) + block.shape[1:])
        bit = (index // distance) % 2
        keep = lax.dynamic_index_in_dim(half, bit, 0, keepdims=False)
        send = lax.dynamic_index_in_dim(half, 1 - bit, 0, keepdims=False)
        route = [(i, i ^ distance) for i in range(count)]
        block = keep + lax.ppermute(send, axis, route)
        distance //= 2
    return block


def doubling_gather(block, axis, count):
    index = lax.axis_index(axis)
    distance = 1
    while distance < count:
        route = [(i, i ^ distance) for i in range(count)]
        other = lax.ppermute(block, axis, route)
        upper = (index // distance) % 2 == 1
        block = jnp.where(
            upper,
            jnp.concatenate([other, block], axis=0),
            jnp.concatenate([block, other], axis=0),
        )
        distance *= 2
    return block


def reduce_all(crossed, decoder_piece, loss_piece, decoder_weight):
    width, variables = crossed.shape
    own = width // TOKENS_AXIS
    lanes = 256
    loss_column = jnp.zeros((width, 1), jnp.float32).at[0, 0].set(loss_piece)
    merged = jnp.concatenate(
        [
            crossed,
            decoder_piece.T,
            loss_column,
            jnp.zeros((width, lanes - 2 * variables - 1), jnp.float32),
        ],
        axis=1,
    )
    merged = merged.reshape(TOK_SHAPE + (own, lanes))
    merged = jnp.transpose(merged, (3, 1, 2, 0, 4, 5)).reshape(-1, lanes)
    for axis in ("core", "x"):
        merged = lax.psum_scatter(merged, axis, scatter_dimension=0, tiled=True)
    merged = halving_scatter(merged, "y", TOK_SHAPE[2])
    merged = halving_scatter(merged, "z_lo", TOK_SHAPE[0])
    merged = doubling_sum(merged, "member", MEMBER_AXIS)
    grad_out = jnp.dot(
        merged[:, :variables],
        decoder_weight.astype(jnp.float32),
        precision=lax.Precision.HIGHEST,
    )
    rest = merged[:, variables : variables + 128]
    rest = lax.all_gather(rest, "core", axis=0, tiled=True)
    rest = doubling_gather(rest, "y", TOK_SHAPE[2])
    for axis in ("x", "z_lo"):
        rest = lax.all_gather(rest, axis, axis=0, tiled=True)
    return grad_out, rest[:, :variables].T, rest[0, variables]


def shards(
    members_in,
    member_noise,
    norm_gain,
    weight_query,
    weight_key,
    weight_value,
    weight_out,
    decoder_projection_weight,
    decoder_bias,
    observations,
    surface_extent_factor,
    quantity_scoring_factor,
    point_map,
):
    member_rows, tokens, width = members_in.shape
    state = members_in.astype(jnp.float32)

    def front(state_in):
        return project(state_in, member_noise, norm_gain, weight_query, weight_key, weight_value)

    (query, key, value), front_pull = jax.vjp(front, state)
    stacked = jnp.stack([key, value])
    extended = extended_2(stacked, ((TOK, 2),), HALF)
    leading_realization = lax.axis_index(TOK) * tokens
    total = tokens * TOKENS_AXIS

    def middle(query_in, extended_in):
        return attend(query_in, extended_in[0], extended_in[1], leading_realization, total)

    attended, middle_pull = jax.vjp(middle, query, extended)
    flat_att = attended.reshape(member_rows * tokens, width)
    update = jnp.dot(flat_att, weight_out, preferred_element_type=jnp.float32).reshape(
        member_rows, tokens, width
    )
    residual_stream_state = (state + member_noise.astype(jnp.float32) + update).astype(jnp.bfloat16)

    def decode_tokens(residual_in, decoder_in):
        mapping_array = jnp.einsum(
            "vc,mtc->mvt",
            decoder_in.astype(jnp.bfloat16),
            residual_in,
            preferred_element_type=jnp.float32,
        )
        return mapping_array + decoder_bias[None, :, None]

    token_prediction, readout_slope_pulled = jax.vjp(
        decode_tokens, residual_stream_state, decoder_projection_weight.astype(jnp.float32)
    )
    location_places = point_map.shape[0]
    groups = lax.axis_size("member")
    local_shard = lax.axis_index("member")
    gathered_tokens = lax.all_gather(token_prediction, "member", axis=0, tiled=True)
    selector = (point_map[:, None] == lax.iota(jnp.int32, tokens)[None, :]).astype(jnp.float32)
    gathered_lines = jnp.einsum(
        "mvt,pt->mvp", gathered_tokens, selector, precision=lax.Precision.HIGHEST
    )

    def score_all(whole):
        return unbiased_ranked_score(
            whole, observations, surface_extent_factor, quantity_scoring_factor
        )

    full_loss, score_pull = jax.vjp(score_all, gathered_lines)
    (complete_gradient,) = score_pull(jnp.ones((), jnp.float32))
    point_slope = lax.dynamic_slice_in_dim(
        complete_gradient, local_shard * member_rows, member_rows, 0
    )
    prediction_slope = jnp.einsum(
        "mvp,pt->mvt", point_slope, selector, precision=lax.Precision.HIGHEST
    )
    partial_loss = full_loss / groups
    carried_slope, readout_piece_result = readout_slope_pulled(prediction_slope)
    flat_grad = carried_slope.reshape(member_rows * tokens, width)
    crossed = jnp.einsum(
        "mtc,mvt->cv",
        attended.astype(jnp.float32),
        prediction_slope,
        precision=lax.Precision.HIGHEST,
    )
    grad_out, grad_decoder, overall_scoring_amount = reduce_all(
        crossed, readout_piece_result, partial_loss, decoder_projection_weight
    )
    mean_scoring = overall_scoring_amount / (
        token_prediction.shape[1] * location_places * TOKENS_AXIS
    )
    grad_attended = (
        jnp.dot(flat_grad, weight_out.T, preferred_element_type=jnp.float32)
        .astype(jnp.bfloat16)
        .reshape(member_rows, tokens, width)
    )
    grad_query, grad_extended = middle_pull(grad_attended)
    lower_rim = grad_extended[:, :, :HALF]
    upper_rim = grad_extended[:, :, tokens + HALF :]
    inner = grad_extended[:, :, HALF : tokens + HALF].astype(jnp.float32)
    from_next = from_behind(lower_rim, TOK, -1)
    from_prev = from_behind(upper_rim, TOK, 1)
    inner = inner.at[:, :, tokens - HALF :].add(from_next.astype(jnp.float32))
    inner = inner.at[:, :, :HALF].add(from_prev.astype(jnp.float32))
    (grad_front,) = front_pull(
        (grad_query, inner[0].astype(jnp.bfloat16), inner[1].astype(jnp.bfloat16))
    )
    grad_members = (grad_front + carried_slope.astype(jnp.float32)).astype(jnp.bfloat16)
    return (mean_scoring, grad_members, grad_out, grad_decoder)


def solution(mesh):
    assert mesh.shape["token"] == TOKENS_AXIS
    assert mesh.shape["member"] == MEMBER_AXIS
    split = Mesh(
        mesh.devices.reshape((mesh.shape["member"],) + TOK_SHAPE), ("member",) + TOK
    )
    return jax.shard_map(
        shards,
        mesh=split,
        in_specs=(
            P("member", TOK, None),
            P("member", TOK, None),
            P(),
            P(),
            P(),
            P(),
            P(),
            P(),
            P(),
            P(None, TOK),
            P(TOK),
            P(),
            P(TOK),
        ),
        out_specs=(P(), P("member", TOK, None), P(TOK, None), P()),
        check_vma=False,
    )
```

```python
import jax
import jax.numpy as jnp
from jax import lax
from jax.sharding import Mesh, PartitionSpec as P


HEADS = 16
HALF = 128
TOK = ("z_lo", "x", "y", "core")
TOK_SHAPE = (2, 4, 4, 2)
TOKENS_AXIS = 64
MEMBER_AXIS = 4


EPSILON = 1e-06
SMOOTH = 0.01


def extended_2(block, sides, width):
    for axis, dim in sides:
        count = TOKENS_AXIS
        forward = [(i, i + 1) for i in range(count - 1)]
        backward = [(target, source) for source, target in forward]
        low = lax.ppermute(
            lax.slice_in_dim(block, block.shape[dim] - width, None, axis=dim), axis, forward
        )
        high = lax.ppermute(lax.slice_in_dim(block, 0, width, axis=dim), axis, backward)
        block = jnp.concatenate([low, block, high], axis=dim)
    return block


def from_behind(block, axis, distance):
    devices = range(TOKENS_AXIS)
    route = [(i - distance, i) for i in devices if i - distance in devices]
    return lax.ppermute(block, axis, route)


def normalize_heads(flat):
    rows, width = flat.shape
    split = flat.reshape(rows, HEADS, width // HEADS)
    split = split * lax.rsqrt(jnp.mean(split * split, axis=-1, keepdims=True) + EPSILON)
    return split.reshape(rows, width)


def project(state_in, member_noise, norm_gain, weight_query, weight_key, weight_value):
    member_rows, tokens, width = state_in.shape
    mixed = state_in + member_noise.astype(jnp.float32)
    normed = (
        mixed * lax.rsqrt(jnp.mean(mixed * mixed, axis=-1, keepdims=True) + EPSILON) * norm_gain
    ).astype(jnp.bfloat16)
    flat = normed.reshape(member_rows * tokens, width)
    query = normalize_heads(jnp.dot(flat, weight_query, preferred_element_type=jnp.float32)).astype(
        jnp.bfloat16
    )
    key = normalize_heads(jnp.dot(flat, weight_key, preferred_element_type=jnp.float32)).astype(
        jnp.bfloat16
    )
    value = jnp.dot(flat, weight_value, preferred_element_type=jnp.float32).astype(jnp.bfloat16)
    full_shape = (member_rows, tokens, width)
    return (query.reshape(full_shape), key.reshape(full_shape), value.reshape(full_shape))


def attend(query, keys, values, leading_realization, total):
    member_rows, queries, width = query.shape
    realization_number = keys.shape[1]
    depth = width // HEADS
    query_heads = query.reshape(member_rows, queries, HEADS, depth)
    key_heads = keys.reshape(member_rows, realization_number, HEADS, depth)
    value_heads = values.reshape(member_rows, realization_number, HEADS, depth)
    scores = jnp.einsum(
        "mqhd,mkhd->mhqk", query_heads, key_heads, preferred_element_type=jnp.float32
    ) / jnp.sqrt(jnp.float32(depth))
    query_pos = leading_realization + lax.iota(jnp.int32, queries)
    key_pos = leading_realization - HALF + lax.iota(jnp.int32, realization_number)
    allowed = (key_pos[None, :] >= query_pos[:, None] - HALF) & (
        key_pos[None, :] < query_pos[:, None] + HALF
    )
    allowed = allowed & (key_pos[None, :] >= 0) & (key_pos[None, :] < total)
    raised = jnp.where(allowed[None, None], jnp.exp(scores), jnp.float32(0.0))
    probs = (raised / jnp.sum(raised, axis=-1, keepdims=True)).astype(jnp.bfloat16)
    mixed = jnp.einsum("mhqk,mkhd->mqhd", probs, value_heads, preferred_element_type=jnp.float32)
    return mixed.reshape(member_rows, queries, width).astype(jnp.bfloat16)


def softened_magnitude(diff):
    return jnp.sqrt(diff * diff + SMOOTH)


def unbiased_ranked_score(
    realization_prediction, observed_grid, surface_extent, quantity_scoring_factor
):
    realization_number = realization_prediction.shape[0]
    accuracy_part = softened_magnitude(realization_prediction[0] - observed_grid)
    for realization_position in range(1, realization_number):
        accuracy_part = accuracy_part + softened_magnitude(
            realization_prediction[realization_position] - observed_grid
        )
    dispersion_part = jnp.zeros_like(accuracy_part)
    for leading_realization in range(realization_number):
        for paired_realization in range(leading_realization + 1, realization_number):
            dispersion_part = dispersion_part + softened_magnitude(
                realization_prediction[leading_realization]
                - realization_prediction[paired_realization]
            )
    score = accuracy_part / realization_number - dispersion_part / (
        realization_number * (realization_number - 1)
    )
    return jnp.sum(quantity_scoring_factor[:, None] * surface_extent[None, :] * score)


def doubling_sum(block, axis, count):
    distance = 1
    while distance < count:
        route = [(i, i ^ distance) for i in range(count)]
        block = block + lax.ppermute(block, axis, route)
        distance *= 2
    return block


def halving_scatter(block, axis, count):
    index = lax.axis_index(axis)
    distance = count // 2
    while distance >= 1:
        half = block.reshape((2, block.shape[0] // 2) + block.shape[1:])
        bit = (index // distance) % 2
        keep = lax.dynamic_index_in_dim(half, bit, 0, keepdims=False)
        send = lax.dynamic_index_in_dim(half, 1 - bit, 0, keepdims=False)
        route = [(i, i ^ distance) for i in range(count)]
        block = keep + lax.ppermute(send, axis, route)
        distance //= 2
    return block


def doubling_gather(block, axis, count):
    index = lax.axis_index(axis)
    distance = 1
    while distance < count:
        route = [(i, i ^ distance) for i in range(count)]
        other = lax.ppermute(block, axis, route)
        upper = (index // distance) % 2 == 1
        block = jnp.where(
            upper,
            jnp.concatenate([other, block], axis=0),
            jnp.concatenate([block, other], axis=0),
        )
        distance *= 2
    return block


def reduce_all(crossed, decoder_piece, loss_piece, decoder_weight):
    width, variables = crossed.shape
    own = width // TOKENS_AXIS
    lanes = 256
    loss_column = jnp.zeros((width, 1), jnp.float32).at[0, 0].set(loss_piece)
    merged = jnp.concatenate(
        [
            crossed,
            decoder_piece.T,
            loss_column,
            jnp.zeros((width, lanes - 2 * variables - 1), jnp.float32),
        ],
        axis=1,
    )
    merged = merged.reshape(TOK_SHAPE + (own, lanes))
    merged = jnp.transpose(merged, (3, 1, 2, 0, 4, 5)).reshape(-1, lanes)
    for axis in ("core", "x"):
        merged = lax.psum_scatter(merged, axis, scatter_dimension=0, tiled=True)
    merged = halving_scatter(merged, "y", TOK_SHAPE[2])
    merged = halving_scatter(merged, "z_lo", TOK_SHAPE[0])
    merged = doubling_sum(merged, "member", MEMBER_AXIS)
    grad_out = jnp.dot(
        merged[:, :variables],
        decoder_weight.astype(jnp.float32),
        precision=lax.Precision.HIGHEST,
    )
    rest = merged[:, variables : variables + 128]
    rest = lax.all_gather(rest, "core", axis=0, tiled=True)
    rest = doubling_gather(rest, "y", TOK_SHAPE[2])
    rest = doubling_gather(rest, "x", TOK_SHAPE[1])
    rest = lax.all_gather(rest, "z_lo", axis=0, tiled=True)
    return grad_out, rest[:, :variables].T, rest[0, variables]


def shards(
    members_in,
    member_noise,
    norm_gain,
    weight_query,
    weight_key,
    weight_value,
    weight_out,
    decoder_projection_weight,
    decoder_bias,
    observations,
    surface_extent_factor,
    quantity_scoring_factor,
    point_map,
):
    member_rows, tokens, width = members_in.shape
    state = members_in.astype(jnp.float32)

    def front(state_in):
        return project(state_in, member_noise, norm_gain, weight_query, weight_key, weight_value)

    (query, key, value), front_pull = jax.vjp(front, state)
    stacked = jnp.stack([key, value])
    extended = extended_2(stacked, ((TOK, 2),), HALF)
    leading_realization = lax.axis_index(TOK) * tokens
    total = tokens * TOKENS_AXIS

    def middle(query_in, extended_in):
        return attend(query_in, extended_in[0], extended_in[1], leading_realization, total)

    attended, middle_pull = jax.vjp(middle, query, extended)
    flat_att = attended.reshape(member_rows * tokens, width)
    update = jnp.dot(flat_att, weight_out, preferred_element_type=jnp.float32).reshape(
        member_rows, tokens, width
    )
    residual_stream_state = (state + member_noise.astype(jnp.float32) + update).astype(jnp.bfloat16)

    def decode_tokens(residual_in, decoder_in):
        mapping_array = jnp.einsum(
            "vc,mtc->mvt",
            decoder_in.astype(jnp.bfloat16),
            residual_in,
            preferred_element_type=jnp.float32,
        )
        return mapping_array + decoder_bias[None, :, None]

    token_prediction, readout_slope_pulled = jax.vjp(
        decode_tokens, residual_stream_state, decoder_projection_weight.astype(jnp.float32)
    )
    location_places = point_map.shape[0]
    groups = lax.axis_size("member")
    local_shard = lax.axis_index("member")
    gathered_tokens = lax.all_gather(token_prediction, "member", axis=0, tiled=True)
    selector = (point_map[:, None] == lax.iota(jnp.int32, tokens)[None, :]).astype(jnp.float32)
    gathered_lines = jnp.einsum(
        "mvt,pt->mvp", gathered_tokens, selector, precision=lax.Precision.HIGHEST
    )

    def score_all(whole):
        return unbiased_ranked_score(
            whole, observations, surface_extent_factor, quantity_scoring_factor
        )

    full_loss, score_pull = jax.vjp(score_all, gathered_lines)
    (complete_gradient,) = score_pull(jnp.ones((), jnp.float32))
    point_slope = lax.dynamic_slice_in_dim(
        complete_gradient, local_shard * member_rows, member_rows, 0
    )
    prediction_slope = jnp.einsum(
        "mvp,pt->mvt", point_slope, selector, precision=lax.Precision.HIGHEST
    )
    partial_loss = full_loss / groups
    carried_slope, readout_piece_result = readout_slope_pulled(prediction_slope)
    flat_grad = carried_slope.reshape(member_rows * tokens, width)
    crossed = jnp.einsum(
        "mtc,mvt->cv",
        attended.astype(jnp.float32),
        prediction_slope,
        precision=lax.Precision.HIGHEST,
    )
    grad_out, grad_decoder, overall_scoring_amount = reduce_all(
        crossed, readout_piece_result, partial_loss, decoder_projection_weight
    )
    mean_scoring = overall_scoring_amount / (
        token_prediction.shape[1] * location_places * TOKENS_AXIS
    )
    grad_attended = (
        jnp.dot(flat_grad, weight_out.T, preferred_element_type=jnp.float32)
        .astype(jnp.bfloat16)
        .reshape(member_rows, tokens, width)
    )
    grad_query, grad_extended = middle_pull(grad_attended)
    lower_rim = grad_extended[:, :, :HALF]
    upper_rim = grad_extended[:, :, tokens + HALF :]
    inner = grad_extended[:, :, HALF : tokens + HALF].astype(jnp.float32)
    from_next = from_behind(lower_rim, TOK, -1)
    from_prev = from_behind(upper_rim, TOK, 1)
    inner = inner.at[:, :, tokens - HALF :].add(from_next.astype(jnp.float32))
    inner = inner.at[:, :, :HALF].add(from_prev.astype(jnp.float32))
    (grad_front,) = front_pull(
        (grad_query, inner[0].astype(jnp.bfloat16), inner[1].astype(jnp.bfloat16))
    )
    grad_members = (grad_front + carried_slope.astype(jnp.float32)).astype(jnp.bfloat16)
    return (mean_scoring, grad_members, grad_out, grad_decoder)


def solution(mesh):
    assert mesh.shape["token"] == TOKENS_AXIS
    assert mesh.shape["member"] == MEMBER_AXIS
    split = Mesh(
        mesh.devices.reshape((mesh.shape["member"],) + TOK_SHAPE), ("member",) + TOK
    )
    return jax.shard_map(
        shards,
        mesh=split,
        in_specs=(
            P("member", TOK, None),
            P("member", TOK, None),
            P(),
            P(),
            P(),
            P(),
            P(),
            P(),
            P(),
            P(None, TOK),
            P(TOK),
            P(),
            P(TOK),
        ),
        out_specs=(P(), P("member", TOK, None), P(TOK, None), P()),
        check_vma=False,
    )
```

```python
import jax
import jax.numpy as jnp
from jax import lax
from jax.sharding import Mesh, PartitionSpec as P


HEADS = 16
HALF = 128
TOK = ("z_lo", "x", "y", "core")
TOK_SHAPE = (2, 4, 4, 2)
TOKENS_AXIS = 64
MEMBER_AXIS = 4


EPSILON = 1e-06
SMOOTH = 0.01


def extended_2(block, sides, width):
    for axis, dim in sides:
        count = TOKENS_AXIS
        forward = [(i, i + 1) for i in range(count - 1)]
        backward = [(target, source) for source, target in forward]
        low = lax.ppermute(
            lax.slice_in_dim(block, block.shape[dim] - width, None, axis=dim), axis, forward
        )
        high = lax.ppermute(lax.slice_in_dim(block, 0, width, axis=dim), axis, backward)
        block = jnp.concatenate([low, block, high], axis=dim)
    return block


def from_behind(block, axis, distance):
    devices = range(TOKENS_AXIS)
    route = [(i - distance, i) for i in devices if i - distance in devices]
    return lax.ppermute(block, axis, route)


def normalize_heads(flat):
    rows, width = flat.shape
    split = flat.reshape(rows, HEADS, width // HEADS)
    split = split * lax.rsqrt(jnp.mean(split * split, axis=-1, keepdims=True) + EPSILON)
    return split.reshape(rows, width)


def project(state_in, member_noise, norm_gain, weight_query, weight_key, weight_value):
    member_rows, tokens, width = state_in.shape
    mixed = state_in + member_noise.astype(jnp.float32)
    normed = (
        mixed * lax.rsqrt(jnp.mean(mixed * mixed, axis=-1, keepdims=True) + EPSILON) * norm_gain
    ).astype(jnp.bfloat16)
    flat = normed.reshape(member_rows * tokens, width)
    query = normalize_heads(jnp.dot(flat, weight_query, preferred_element_type=jnp.float32)).astype(
        jnp.bfloat16
    )
    key = normalize_heads(jnp.dot(flat, weight_key, preferred_element_type=jnp.float32)).astype(
        jnp.bfloat16
    )
    value = jnp.dot(flat, weight_value, preferred_element_type=jnp.float32).astype(jnp.bfloat16)
    full_shape = (member_rows, tokens, width)
    return (query.reshape(full_shape), key.reshape(full_shape), value.reshape(full_shape))


def attend(query, keys, values, leading_realization, total):
    member_rows, queries, width = query.shape
    realization_number = keys.shape[1]
    depth = width // HEADS
    query_heads = query.reshape(member_rows, queries, HEADS, depth)
    key_heads = keys.reshape(member_rows, realization_number, HEADS, depth)
    value_heads = values.reshape(member_rows, realization_number, HEADS, depth)
    scores = jnp.einsum(
        "mqhd,mkhd->mhqk", query_heads, key_heads, preferred_element_type=jnp.float32
    ) / jnp.sqrt(jnp.float32(depth))
    query_pos = leading_realization + lax.iota(jnp.int32, queries)
    key_pos = leading_realization - HALF + lax.iota(jnp.int32, realization_number)
    allowed = (key_pos[None, :] >= query_pos[:, None] - HALF) & (
        key_pos[None, :] < query_pos[:, None] + HALF
    )
    allowed = allowed & (key_pos[None, :] >= 0) & (key_pos[None, :] < total)
    raised = jnp.where(allowed[None, None], jnp.exp(scores), jnp.float32(0.0))
    probs = (raised / jnp.sum(raised, axis=-1, keepdims=True)).astype(jnp.bfloat16)
    mixed = jnp.einsum("mhqk,mkhd->mqhd", probs, value_heads, preferred_element_type=jnp.float32)
    return mixed.reshape(member_rows, queries, width).astype(jnp.bfloat16)


def softened_magnitude(diff):
    return jnp.sqrt(diff * diff + SMOOTH)


def unbiased_ranked_score(
    realization_prediction, observed_grid, surface_extent, quantity_scoring_factor
):
    realization_number = realization_prediction.shape[0]
    accuracy_part = softened_magnitude(realization_prediction[0] - observed_grid)
    for realization_position in range(1, realization_number):
        accuracy_part = accuracy_part + softened_magnitude(
            realization_prediction[realization_position] - observed_grid
        )
    dispersion_part = jnp.zeros_like(accuracy_part)
    for leading_realization in range(realization_number):
        for paired_realization in range(leading_realization + 1, realization_number):
            dispersion_part = dispersion_part + softened_magnitude(
                realization_prediction[leading_realization]
                - realization_prediction[paired_realization]
            )
    score = accuracy_part / realization_number - dispersion_part / (
        realization_number * (realization_number - 1)
    )
    return jnp.sum(quantity_scoring_factor[:, None] * surface_extent[None, :] * score)


def doubling_sum(block, axis, count):
    distance = 1
    while distance < count:
        route = [(i, i ^ distance) for i in range(count)]
        block = block + lax.ppermute(block, axis, route)
        distance *= 2
    return block


def halving_scatter(block, axis, count):
    index = lax.axis_index(axis)
    distance = count // 2
    while distance >= 1:
        half = block.reshape((2, block.shape[0] // 2) + block.shape[1:])
        bit = (index // distance) % 2
        keep = lax.dynamic_index_in_dim(half, bit, 0, keepdims=False)
        send = lax.dynamic_index_in_dim(half, 1 - bit, 0, keepdims=False)
        route = [(i, i ^ distance) for i in range(count)]
        block = keep + lax.ppermute(send, axis, route)
        distance //= 2
    return block


def doubling_gather(block, axis, count):
    index = lax.axis_index(axis)
    distance = 1
    while distance < count:
        route = [(i, i ^ distance) for i in range(count)]
        other = lax.ppermute(block, axis, route)
        upper = (index // distance) % 2 == 1
        block = jnp.where(
            upper,
            jnp.concatenate([other, block], axis=0),
            jnp.concatenate([block, other], axis=0),
        )
        distance *= 2
    return block


def reduce_all(crossed, decoder_piece, loss_piece, decoder_weight):
    width, variables = crossed.shape
    own = width // TOKENS_AXIS
    lanes = 256
    loss_column = jnp.zeros((width, 1), jnp.float32).at[0, 0].set(loss_piece)
    merged = jnp.concatenate(
        [
            crossed,
            decoder_piece.T,
            loss_column,
            jnp.zeros((width, lanes - 2 * variables - 1), jnp.float32),
        ],
        axis=1,
    )
    merged = merged.reshape(TOK_SHAPE + (own, lanes))
    merged = jnp.transpose(merged, (3, 1, 2, 0, 4, 5)).reshape(-1, lanes)
    for axis in ("core", "x"):
        merged = lax.psum_scatter(merged, axis, scatter_dimension=0, tiled=True)
    merged = halving_scatter(merged, "y", TOK_SHAPE[2])
    merged = halving_scatter(merged, "z_lo", TOK_SHAPE[0])
    merged = doubling_sum(merged, "member", MEMBER_AXIS)
    grad_out = jnp.dot(
        merged[:, :variables],
        decoder_weight.astype(jnp.float32),
        precision=lax.Precision.HIGHEST,
    )
    rest = merged[:, variables : variables + 128]
    rest = lax.all_gather(rest, "core", axis=0, tiled=True)
    rest = doubling_gather(rest, "y", TOK_SHAPE[2])
    rest = doubling_gather(rest, "x", TOK_SHAPE[1])
    rest = doubling_gather(rest, "z_lo", TOK_SHAPE[0])
    return grad_out, rest[:, :variables].T, rest[0, variables]


def shards(
    members_in,
    member_noise,
    norm_gain,
    weight_query,
    weight_key,
    weight_value,
    weight_out,
    decoder_projection_weight,
    decoder_bias,
    observations,
    surface_extent_factor,
    quantity_scoring_factor,
    point_map,
):
    member_rows, tokens, width = members_in.shape
    state = members_in.astype(jnp.float32)

    def front(state_in):
        return project(state_in, member_noise, norm_gain, weight_query, weight_key, weight_value)

    (query, key, value), front_pull = jax.vjp(front, state)
    stacked = jnp.stack([key, value])
    extended = extended_2(stacked, ((TOK, 2),), HALF)
    leading_realization = lax.axis_index(TOK) * tokens
    total = tokens * TOKENS_AXIS

    def middle(query_in, extended_in):
        return attend(query_in, extended_in[0], extended_in[1], leading_realization, total)

    attended, middle_pull = jax.vjp(middle, query, extended)
    flat_att = attended.reshape(member_rows * tokens, width)
    update = jnp.dot(flat_att, weight_out, preferred_element_type=jnp.float32).reshape(
        member_rows, tokens, width
    )
    residual_stream_state = (state + member_noise.astype(jnp.float32) + update).astype(jnp.bfloat16)

    def decode_tokens(residual_in, decoder_in):
        mapping_array = jnp.einsum(
            "vc,mtc->mvt",
            decoder_in.astype(jnp.bfloat16),
            residual_in,
            preferred_element_type=jnp.float32,
        )
        return mapping_array + decoder_bias[None, :, None]

    token_prediction, readout_slope_pulled = jax.vjp(
        decode_tokens, residual_stream_state, decoder_projection_weight.astype(jnp.float32)
    )
    location_places = point_map.shape[0]
    groups = lax.axis_size("member")
    local_shard = lax.axis_index("member")
    gathered_tokens = lax.all_gather(token_prediction, "member", axis=0, tiled=True)
    selector = (point_map[:, None] == lax.iota(jnp.int32, tokens)[None, :]).astype(jnp.float32)
    gathered_lines = jnp.einsum(
        "mvt,pt->mvp", gathered_tokens, selector, precision=lax.Precision.HIGHEST
    )

    def score_all(whole):
        return unbiased_ranked_score(
            whole, observations, surface_extent_factor, quantity_scoring_factor
        )

    full_loss, score_pull = jax.vjp(score_all, gathered_lines)
    (complete_gradient,) = score_pull(jnp.ones((), jnp.float32))
    point_slope = lax.dynamic_slice_in_dim(
        complete_gradient, local_shard * member_rows, member_rows, 0
    )
    prediction_slope = jnp.einsum(
        "mvp,pt->mvt", point_slope, selector, precision=lax.Precision.HIGHEST
    )
    partial_loss = full_loss / groups
    carried_slope, readout_piece_result = readout_slope_pulled(prediction_slope)
    flat_grad = carried_slope.reshape(member_rows * tokens, width)
    crossed = jnp.einsum(
        "mtc,mvt->cv",
        attended.astype(jnp.float32),
        prediction_slope,
        precision=lax.Precision.HIGHEST,
    )
    grad_out, grad_decoder, overall_scoring_amount = reduce_all(
        crossed, readout_piece_result, partial_loss, decoder_projection_weight
    )
    mean_scoring = overall_scoring_amount / (
        token_prediction.shape[1] * location_places * TOKENS_AXIS
    )
    grad_attended = (
        jnp.dot(flat_grad, weight_out.T, preferred_element_type=jnp.float32)
        .astype(jnp.bfloat16)
        .reshape(member_rows, tokens, width)
    )
    grad_query, grad_extended = middle_pull(grad_attended)
    lower_rim = grad_extended[:, :, :HALF]
    upper_rim = grad_extended[:, :, tokens + HALF :]
    inner = grad_extended[:, :, HALF : tokens + HALF].astype(jnp.float32)
    from_next = from_behind(lower_rim, TOK, -1)
    from_prev = from_behind(upper_rim, TOK, 1)
    inner = inner.at[:, :, tokens - HALF :].add(from_next.astype(jnp.float32))
    inner = inner.at[:, :, :HALF].add(from_prev.astype(jnp.float32))
    (grad_front,) = front_pull(
        (grad_query, inner[0].astype(jnp.bfloat16), inner[1].astype(jnp.bfloat16))
    )
    grad_members = (grad_front + carried_slope.astype(jnp.float32)).astype(jnp.bfloat16)
    return (mean_scoring, grad_members, grad_out, grad_decoder)


def solution(mesh):
    assert mesh.shape["token"] == TOKENS_AXIS
    assert mesh.shape["member"] == MEMBER_AXIS
    split = Mesh(
        mesh.devices.reshape((mesh.shape["member"],) + TOK_SHAPE), ("member",) + TOK
    )
    return jax.shard_map(
        shards,
        mesh=split,
        in_specs=(
            P("member", TOK, None),
            P("member", TOK, None),
            P(),
            P(),
            P(),
            P(),
            P(),
            P(),
            P(),
            P(None, TOK),
            P(TOK),
            P(),
            P(TOK),
        ),
        out_specs=(P(), P("member", TOK, None), P(TOK, None), P()),
        check_vma=False,
    )
```
